32 devices in a mesh: ens: 2 (over y), lon: 8 (over z, x), lat: 2 (over core).
Axes of the slice: x: 2, y: 2, z: 4, core: 2. Of those that a mesh axis runs over, the one named last changes fastest.
Arguments:
- control: float32 [4, 2, 256, 512], P('ens', None, 'lon', 'lat'), parts along dimension 0, may hold values from -6 to 6
- error_std: float32 [2, 2, 256, 512], P(None, None, 'lon', 'lat'), may hold values from 0.5 to 2
- land_mask: int32 [2, 256, 512], P(None, 'lon', 'lat'), may hold values 0 or 1
- diff_east: float32 [256, 512], P('lon', 'lat'), may hold values from 0.02 to 0.12
- diff_north: float32 [256, 512], P('lon', 'lat'), may hold values from 0.02 to 0.12
- fold_partner: int32 [256], replicated, may hold values from 0 to 255, as said below
Outputs:
- gradient: float32 [4, 2, 256, 512], P('ens', None, 'lon', 'lat'), parts along dimension 0
The draws below stay inside these ranges and needn't reach their ends.
There are 2 independent parts, one for each index of `ens`. The reference program is written for one: setup_inputs(seed, part) draws one part's arguments, and reference() takes and returns one part's arrays. A program takes and returns all parts, laid end to end along the dimension named above; an argument that names none is the same for every part. Nothing has to cross between parts.
Inputs may be any that keep to these rules, and one draw needn't show every extreme that they name: fold_partner[i] = (s - i) modulo 256 for one pivot s drawn from the seed, so fold_partner[fold_partner[i]] = i.
All inputs are finite; a program needn't handle non-finite values. No bound on the sum of `land_mask` on one device may be relied on, other than what follows from the above.
Results may differ from the reference program's by a relative error of at most 0.00002.
Values sent between devices are 32-bit elements; how exact they have to be, the bound alone decides.
No kernel may reach another device: no remote copies, remote signals or barrier semaphores. Data moves between devices by JAX's collectives and lax.ppermute only.
A program may use at most 64 MiB of HBM per device.

```python
import math
import jax
import jax.numpy as jnp

VARS = 2
LEV = 2
STEPS = 8
NLON = 256
NLAT = 512


def draw_fold_partner(key, part):
    pivot = jax.random.randint(key, (), 0, NLON)
    places = jnp.arange(NLON, dtype=jnp.int32)
    return ((pivot - places) % NLON).astype(jnp.int32)


def with_ends(drawn, own_key, smallest, largest):
    spot = [jax.random.randint(jax.random.fold_in(own_key, axis), (), 0, length) for axis, length in enumerate(drawn.shape)]
    longest = drawn.shape.index(max(drawn.shape))
    next_to = spot[:longest] + [(spot[longest] + 1) % drawn.shape[longest]] + spot[longest + 1:]
    return drawn.at[tuple(spot)].set(smallest).at[tuple(next_to)].set(largest)


def steps_of(key, shape, cuts, low, largest):
    loudness, own = 1.0, jax.random.fold_in(key, 6)
    for dim, parts in cuts:
        steps = jnp.exp(jax.random.uniform(jax.random.fold_in(own, dim), (parts,), jnp.float32, low / len(cuts), largest / len(cuts)))
        loudness = loudness * jnp.repeat(steps, shape[dim] // parts).reshape([-1 if axis == dim else 1 for axis in range(len(shape))])
    return loudness


def centred(rng, shape, deviation, most, pieces=(), held_as=jnp.bfloat16):
    entries = jax.random.normal(rng, shape, jnp.float32) * deviation
    if len(pieces) > 0:
        entries = steps_of(rng, shape, pieces, -0.22, 0.18) * entries
    return jnp.clip(entries, min=-most, max=most).astype(held_as)


def setup_inputs(seed: int = 0, part: int = 0) -> dict:
    splits = jax.random.split(jax.random.key(seed), 7)
    part_keys = jax.random.split(jax.random.fold_in(splits[6], part), 7)
    control = centred(part_keys[0], (VARS, LEV, NLON, NLAT), 1.0, 6.0, ((2, 8), (3, 2)), jnp.float32)
    error_std = jnp.clip(jnp.exp(math.log(2.0) - 1.3862944 * jax.random.uniform(splits[1], (VARS, LEV, NLON, NLAT), jnp.float32) ** steps_of(splits[1], (VARS, LEV, NLON, NLAT), ((2, 8), (3, 2)), -0.2, 0.2)), 0.5, 2.0)
    land_mask = with_ends((jax.random.randint(splits[2], (LEV, NLON, NLAT), 0, 4) < 3).astype(jnp.int32), jax.random.fold_in(splits[2], 1), 0, 1)
    diff_east = jnp.clip(jnp.exp(math.log(0.12) - 1.7917595 * jax.random.uniform(splits[3], (NLON, NLAT), jnp.float32) ** steps_of(splits[3], (NLON, NLAT), ((0, 8), (1, 2)), -0.2, 0.2)), 0.02, 0.12)
    diff_north = jnp.clip(jnp.exp(math.log(0.12) - 1.7917595 * jax.random.uniform(splits[4], (NLON, NLAT), jnp.float32) ** steps_of(splits[4], (NLON, NLAT), ((0, 8), (1, 2)), -0.2, 0.2)), 0.02, 0.12)
    fold_partner = draw_fold_partner(jax.random.fold_in(splits[6], 71), part)
    return {"control": control, "error_std": error_std, "land_mask": land_mask, "diff_east": diff_east, "diff_north": diff_north, "fold_partner": fold_partner}


def diffuse(current, mask_float, diff_east, diff_north, fold_partner):
    east_next = jnp.roll(current, -1, axis=2)
    mask_next = jnp.roll(mask_float, -1, axis=1)
    east_flux = diff_east * mask_float * mask_next * (east_next - current)
    east_change = east_flux - jnp.roll(east_flux, 1, axis=2)
    north_flux = diff_north[:, :-1] * mask_float[:, :, :-1] * mask_float[:, :, 1:] * (current[..., 1:] - current[..., :-1])
    zero_row = jnp.zeros(current.shape[:3] + (1,), jnp.float32)
    north_change = jnp.concatenate([north_flux, zero_row], axis=3) - jnp.concatenate([zero_row, north_flux], axis=3)
    top_row = current[..., -1]
    mirrored = top_row[:, :, fold_partner]
    top_mask = mask_float[:, :, -1]
    mate_mask = top_mask[:, fold_partner]
    top_kappa = diff_north[:, -1]
    mate_kappa = top_kappa[fold_partner]
    fold_change = 0.5 * (top_kappa + mate_kappa) * top_mask * mate_mask * (mirrored - top_row)
    rest = jnp.zeros(current.shape[:3] + (current.shape[3] - 1,), jnp.float32)
    fold_full = jnp.concatenate([rest, fold_change[..., None]], axis=3)
    return current + east_change + north_change + fold_full


def reference(control, error_std, land_mask, diff_east, diff_north, fold_partner):
    mask_float = land_mask.astype(jnp.float32)
    current = error_std * control
    for sweep in range(STEPS):
        current = diffuse(current, mask_float, diff_east, diff_north, fold_partner)
    return error_std * current
```

```python
import jax
import jax.numpy as jnp
from jax import lax
from jax.sharding import PartitionSpec as P

STEPS = 8


def halo_pair(x, axis, dim, width, wrap):
    peers, length = lax.axis_size(axis), x.shape[dim]
    up = [(i, (i + 1) % peers) for i in range(peers if wrap else peers - 1)]
    down = [(j, i) for i, j in up]
    last = lax.slice_in_dim(x, length - width, length, axis=dim)
    first = lax.slice_in_dim(x, 0, width, axis=dim)
    return lax.ppermute(last, axis, up), lax.ppermute(first, axis, down)


def gather_lon(strip, own_start):
    peers = lax.axis_size("lon")
    if peers > 16:
        return lax.all_gather(strip, "lon", axis=1, tiled=True), 0
    parts = [strip]
    for q in range(1, peers):
        pairs = [(i, (i - q) % peers) for i in range(peers)]
        parts.append(lax.ppermute(strip, "lon", pairs))
    return jnp.concatenate(parts, axis=1), own_start


def per_device(control, error_std, land_mask, diff_east, diff_north, fold_partner):
    nvar, nlev, cells_lon, cells_lat = control.shape
    depth = STEPS
    nlon = fold_partner.shape[0]
    width = cells_lon + 2 * depth
    rows = cells_lat + 2 * depth
    nfield = nvar * nlev
    lat_index, lat_peers = lax.axis_index("lat"), lax.axis_size("lat")
    is_top = lat_index == lat_peers - 1
    is_bottom = lat_index == 0
    col0 = lax.axis_index("lon") * cells_lon

    field = (error_std * control).reshape(nfield, cells_lon, cells_lat)
    stack = jnp.concatenate(
        [field, land_mask.astype(jnp.float32), diff_east[None], diff_north[None]], axis=0
    )

    strip = stack[:, :, cells_lat - depth :]
    gathered, base = gather_lon(strip, col0)
    pivot = fold_partner[0]
    first = (pivot - col0 - cells_lon - depth + 1 - base) % nlon
    doubled = jnp.concatenate([gathered, gathered[:, :width]], axis=1)
    mirror = lax.dynamic_slice_in_dim(doubled, first, width, axis=1)[:, ::-1, ::-1]

    west, east = halo_pair(stack, "lon", 1, depth, True)
    wide = jnp.concatenate([west, stack, east], axis=1)
    south, north = halo_pair(wide, "lat", 2, depth, False)
    north = jnp.where(is_top, mirror, north)
    ext = jnp.concatenate([south, wide, north], axis=2)

    mask = ext[nfield : nfield + nlev]
    kappa_e = ext[nfield + nlev]
    kappa_n = ext[nfield + nlev + 1]
    r = jnp.arange(rows, dtype=jnp.int32)
    virtual = (is_top & (r >= depth + cells_lat))[None, :]
    fold_row = (is_top & (r == depth + cells_lat - 1))[None, :]
    south_edge = (is_bottom & (r < depth))[None, :]
    kappa_e = jnp.where(virtual, jnp.roll(kappa_e, -1, axis=0), kappa_e)
    kappa_up = jnp.roll(kappa_n, -1, axis=1)
    kappa_n = jnp.where(
        virtual, kappa_up, jnp.where(fold_row, 0.5 * (kappa_n + kappa_up), kappa_n)
    )
    coef_e = kappa_e * mask * jnp.roll(mask, -1, axis=1)
    coef_n = kappa_n * mask * jnp.roll(mask, -1, axis=2)
    coef_n = jnp.where(south_edge[None], 0.0, coef_n)

    v = ext[:nfield].reshape(nvar, nlev, width, rows)
    for sweep in range(STEPS):
        flux_e = coef_e * (jnp.roll(v, -1, axis=2) - v)
        flux_n = coef_n * (jnp.roll(v, -1, axis=3) - v)
        v = v + (flux_e - jnp.roll(flux_e, 1, axis=2)) + (flux_n - jnp.roll(flux_n, 1, axis=3))
    own = v[:, :, depth : depth + cells_lon, depth : depth + cells_lat]
    return error_std * own


def solution(mesh):
    return jax.shard_map(
        per_device,
        mesh=mesh,
        in_specs=(
            P("ens", None, "lon", "lat"),
            P(None, None, "lon", "lat"),
            P(None, "lon", "lat"),
            P("lon", "lat"),
            P("lon", "lat"),
            P(),
        ),
        out_specs=P("ens", None, "lon", "lat"),
        check_vma=False,
    )
```

```python
import jax
import jax.numpy as jnp
from jax import lax
from jax.sharding import PartitionSpec as P

STEPS = 8


AXES = ("lon", "lat")


def exchange(sends):
    groups = {}
    for k, (pairs, x) in enumerate(sends):
        groups.setdefault(tuple(pairs), []).append(k)
    out = [None] * len(sends)
    for pairs, members in groups.items():
        if len(members) == 1:
            out[members[0]] = lax.ppermute(sends[members[0]][1], AXES, list(pairs))
            continue
        flat = jnp.concatenate([sends[k][1].reshape(-1) for k in members])
        got = lax.ppermute(flat, AXES, list(pairs))
        offset = 0
        for k in members:
            size = sends[k][1].size
            out[k] = got[offset : offset + size].reshape(sends[k][1].shape)
            offset += size
    return out


def pairs_from(d_lon, d_lat):
    nlon, nlat = lax.axis_size("lon"), lax.axis_size("lat")
    pairs = []
    for lon in range(nlon):
        for lat in range(nlat):
            dst = lat - d_lat
            if 0 <= dst < nlat:
                pairs.append((lon * nlat + lat, ((lon - d_lon) % nlon) * nlat + dst))
    return pairs


def per_device(control, error_std, land_mask, diff_east, diff_north, fold_partner):
    nvar, nlev, cells_lon, cells_lat = control.shape
    depth = STEPS
    nlon = fold_partner.shape[0]
    width = cells_lon + 2 * depth
    rows = cells_lat + 2 * depth
    nfield = nvar * nlev
    lat_index, lat_peers = lax.axis_index("lat"), lax.axis_size("lat")
    is_top = lat_index == lat_peers - 1
    is_bottom = lat_index == 0
    col0 = lax.axis_index("lon") * cells_lon

    field = (error_std * control).reshape(nfield, cells_lon, cells_lat)
    stack = jnp.concatenate(
        [field, land_mask.astype(jnp.float32), diff_east[None], diff_north[None]], axis=0
    )

    nlon_dev = lax.axis_size("lon")
    d = depth
    top, bottom = stack[:, :, cells_lat - d :], stack[:, :, :d]
    left, right = stack[:, :d], stack[:, cells_lon - d :]
    sends = [
        (pairs_from(-1, 0), right),
        (pairs_from(1, 0), left),
        (pairs_from(0, -1), top),
        (pairs_from(0, 1), bottom),
        (pairs_from(-1, -1), right[:, :, cells_lat - d :]),
        (pairs_from(1, -1), left[:, :, cells_lat - d :]),
        (pairs_from(-1, 1), right[:, :, :d]),
        (pairs_from(1, 1), left[:, :, :d]),
    ]
    small = nlon_dev <= 16
    if small:
        sends += [(pairs_from(q, 0), top) for q in range(1, nlon_dev)]
    got = exchange(sends)
    west, east, south, north, sw, se, nw, ne = got[:8]

    if small:
        gathered, base = jnp.concatenate([top] + got[8:], axis=1), col0
    else:
        gathered, base = lax.all_gather(top, "lon", axis=1, tiled=True), 0
    pivot = fold_partner[0]
    first = (pivot - col0 - cells_lon - depth + 1 - base) % nlon
    doubled = jnp.concatenate([gathered, gathered[:, :width]], axis=1)
    mirror = lax.dynamic_slice_in_dim(doubled, first, width, axis=1)[:, ::-1, ::-1]

    south_band = jnp.concatenate([sw, south, se], axis=1)
    north_band = jnp.concatenate([nw, north, ne], axis=1)
    north_band = jnp.where(is_top, mirror, north_band)
    wide = jnp.concatenate([west, stack, east], axis=1)
    ext = jnp.concatenate([south_band, wide, north_band], axis=2)

    mask = ext[nfield : nfield + nlev]
    kappa_e = ext[nfield + nlev]
    kappa_n = ext[nfield + nlev + 1]
    r = jnp.arange(rows, dtype=jnp.int32)
    virtual = (is_top & (r >= depth + cells_lat))[None, :]
    fold_row = (is_top & (r == depth + cells_lat - 1))[None, :]
    south_edge = (is_bottom & (r < depth))[None, :]
    kappa_e = jnp.where(virtual, jnp.roll(kappa_e, -1, axis=0), kappa_e)
    kappa_up = jnp.roll(kappa_n, -1, axis=1)
    kappa_n = jnp.where(
        virtual, kappa_up, jnp.where(fold_row, 0.5 * (kappa_n + kappa_up), kappa_n)
    )
    coef_e = kappa_e * mask * jnp.roll(mask, -1, axis=1)
    coef_n = kappa_n * mask * jnp.roll(mask, -1, axis=2)
    coef_n = jnp.where(south_edge[None], 0.0, coef_n)

    v = ext[:nfield].reshape(nvar, nlev, width, rows)
    for sweep in range(STEPS):
        flux_e = coef_e * (jnp.roll(v, -1, axis=2) - v)
        flux_n = coef_n * (jnp.roll(v, -1, axis=3) - v)
        v = v + (flux_e - jnp.roll(flux_e, 1, axis=2)) + (flux_n - jnp.roll(flux_n, 1, axis=3))
    own = v[:, :, depth : depth + cells_lon, depth : depth + cells_lat]
    return error_std * own


def solution(mesh):
    return jax.shard_map(
        per_device,
        mesh=mesh,
        in_specs=(
            P("ens", None, "lon", "lat"),
            P(None, None, "lon", "lat"),
            P(None, "lon", "lat"),
            P("lon", "lat"),
            P("lon", "lat"),
            P(),
        ),
        out_specs=P("ens", None, "lon", "lat"),
        check_vma=False,
    )
```

```python
import jax
import jax.numpy as jnp
from jax import lax
from jax.sharding import PartitionSpec as P

STEPS = 8


AXES = ("lon", "lat")


def exchange(sends):
    groups = {}
    for k, (pairs, x) in enumerate(sends):
        groups.setdefault(tuple(pairs), []).append(k)
    out = [None] * len(sends)
    for pairs, members in groups.items():
        if len(members) == 1:
            out[members[0]] = lax.ppermute(sends[members[0]][1], AXES, list(pairs))
            continue
        flat = jnp.concatenate([sends[k][1].reshape(-1) for k in members])
        got = lax.ppermute(flat, AXES, list(pairs))
        offset = 0
        for k in members:
            size = sends[k][1].size
            out[k] = got[offset : offset + size].reshape(sends[k][1].shape)
            offset += size
    return out


def pairs_from(d_lon, d_lat):
    nlon, nlat = lax.axis_size("lon"), lax.axis_size("lat")
    pairs = []
    for lon in range(nlon):
        for lat in range(nlat):
            dst = lat - d_lat
            if 0 <= dst < nlat:
                pairs.append((lon * nlat + lat, ((lon - d_lon) % nlon) * nlat + dst))
    return pairs


def per_device(control, error_std, land_mask, diff_east, diff_north, fold_partner):
    nvar, nlev, cells_lon, cells_lat = control.shape
    depth = STEPS
    nlon = fold_partner.shape[0]
    width = cells_lon + 2 * depth
    rows = cells_lat + 2 * depth
    nfield = nvar * nlev
    lat_index, lat_peers = lax.axis_index("lat"), lax.axis_size("lat")
    is_top = lat_index == lat_peers - 1
    is_bottom = lat_index == 0
    col0 = lax.axis_index("lon") * cells_lon

    field = (error_std * control).reshape(nfield, cells_lon, cells_lat)
    stack = jnp.concatenate(
        [field, land_mask.astype(jnp.float32), diff_east[None], diff_north[None]], axis=0
    )

    nlon_dev = lax.axis_size("lon")
    d = depth
    top = stack[:, :, cells_lat - d :]
    small = nlon_dev <= 16
    west, east, from_west, from_east = exchange(
        [
            (pairs_from(-1, 0), stack[:, cells_lon - d :]),
            (pairs_from(1, 0), stack[:, :d]),
            (pairs_from(-1, 0), top),
            (pairs_from(1, 0), top),
        ]
    )
    wide = jnp.concatenate([west, stack, east], axis=1)
    window, span = jnp.concatenate([from_west, top, from_east], axis=1), 3
    sends = [(pairs_from(0, -1), wide[:, :, cells_lat - d :]), (pairs_from(0, 1), wide[:, :, :d])]
    while small and span < nlon_dev:
        sends += [(pairs_from(-span, 0), window), (pairs_from(span, 0), window)]
        got = exchange(sends)
        window = jnp.concatenate([got[-2], window, got[-1]], axis=1)
        span, sends = 3 * span, []
        if len(got) == 4:
            south, north = got[:2]
    if sends:
        south, north = exchange(sends)

    if small:
        gathered, base = window, col0 - (span // 2) * cells_lon
    else:
        gathered, base = lax.all_gather(top, "lon", axis=1, tiled=True), 0
    pivot = fold_partner[0]
    first = (pivot - col0 - cells_lon - depth + 1 - base) % nlon
    doubled = jnp.concatenate([gathered[:, :nlon], gathered[:, :width]], axis=1)
    mirror = lax.dynamic_slice_in_dim(doubled, first, width, axis=1)[:, ::-1, ::-1]

    south_band, north_band = south, north
    north_band = jnp.where(is_top, mirror, north_band)
    ext = jnp.concatenate([south_band, wide, north_band], axis=2)

    mask = ext[nfield : nfield + nlev]
    kappa_e = ext[nfield + nlev]
    kappa_n = ext[nfield + nlev + 1]
    r = jnp.arange(rows, dtype=jnp.int32)
    virtual = (is_top & (r >= depth + cells_lat))[None, :]
    fold_row = (is_top & (r == depth + cells_lat - 1))[None, :]
    south_edge = (is_bottom & (r < depth))[None, :]
    kappa_e = jnp.where(virtual, jnp.roll(kappa_e, -1, axis=0), kappa_e)
    kappa_up = jnp.roll(kappa_n, -1, axis=1)
    kappa_n = jnp.where(
        virtual, kappa_up, jnp.where(fold_row, 0.5 * (kappa_n + kappa_up), kappa_n)
    )
    coef_e = kappa_e * mask * jnp.roll(mask, -1, axis=1)
    coef_n = kappa_n * mask * jnp.roll(mask, -1, axis=2)
    coef_n = jnp.where(south_edge[None], 0.0, coef_n)

    v = ext[:nfield].reshape(nvar, nlev, width, rows)
    for sweep in range(STEPS):
        flux_e = coef_e * (jnp.roll(v, -1, axis=2) - v)
        flux_n = coef_n * (jnp.roll(v, -1, axis=3) - v)
        v = v + (flux_e - jnp.roll(flux_e, 1, axis=2)) + (flux_n - jnp.roll(flux_n, 1, axis=3))
    own = v[:, :, depth : depth + cells_lon, depth : depth + cells_lat]
    return error_std * own


def solution(mesh):
    return jax.shard_map(
        per_device,
        mesh=mesh,
        in_specs=(
            P("ens", None, "lon", "lat"),
            P(None, None, "lon", "lat"),
            P(None, "lon", "lat"),
            P("lon", "lat"),
            P("lon", "lat"),
            P(),
        ),
        out_specs=P("ens", None, "lon", "lat"),
        check_vma=False,
    )
```

```python
import jax
import jax.numpy as jnp
from jax import lax
from jax.sharding import PartitionSpec as P

STEPS = 8


AXES = ("lon", "lat")


def exchange(sends):
    groups = {}
    for k, (pairs, x) in enumerate(sends):
        groups.setdefault(tuple(pairs), []).append(k)
    out = [None] * len(sends)
    for pairs, members in groups.items():
        if len(members) == 1:
            out[members[0]] = lax.ppermute(sends[members[0]][1], AXES, list(pairs))
            continue
        flat = jnp.concatenate([sends[k][1].reshape(-1) for k in members])
        got = lax.ppermute(flat, AXES, list(pairs))
        offset = 0
        for k in members:
            size = sends[k][1].size
            out[k] = got[offset : offset + size].reshape(sends[k][1].shape)
            offset += size
    return out


def pairs_from(d_lon, d_lat):
    nlon, nlat = lax.axis_size("lon"), lax.axis_size("lat")
    pairs = []
    for lon in range(nlon):
        for lat in range(nlat):
            dst = lat - d_lat
            if 0 <= dst < nlat:
                pairs.append((lon * nlat + lat, ((lon - d_lon) % nlon) * nlat + dst))
    return pairs


def per_device(control, error_std, land_mask, diff_east, diff_north, fold_partner):
    nvar, nlev, cells_lon, cells_lat = control.shape
    depth = STEPS
    nlon = fold_partner.shape[0]
    width = cells_lon + 2 * depth
    rows = cells_lat + 2 * depth
    nfield = nvar * nlev
    lat_index, lat_peers = lax.axis_index("lat"), lax.axis_size("lat")
    is_top = lat_index == lat_peers - 1
    is_bottom = lat_index == 0
    col0 = lax.axis_index("lon") * cells_lon

    def planes(cols, rows):
        field = error_std[:, :, cols, rows] * control[:, :, cols, rows]
        return jnp.concatenate(
            [
                field.reshape((nfield,) + field.shape[2:]),
                land_mask[:, cols, rows].astype(jnp.float32),
                diff_east[None, cols, rows],
                diff_north[None, cols, rows],
            ],
            axis=0,
        )

    nlon_dev = lax.axis_size("lon")
    d = depth
    every = slice(None)
    top = planes(every, slice(cells_lat - d, None))
    small = nlon_dev <= 16
    west, east, from_west, from_east = exchange(
        [
            (pairs_from(-1, 0), planes(slice(cells_lon - d, None), every)),
            (pairs_from(1, 0), planes(slice(0, d), every)),
            (pairs_from(-1, 0), top),
            (pairs_from(1, 0), top),
        ]
    )
    stack = planes(every, every)
    wide = jnp.concatenate([west, stack, east], axis=1)
    window, span = jnp.concatenate([from_west, top, from_east], axis=1), 3
    if lat_peers == 2:
        facing = jnp.where(is_top, wide[:, :, :d], wide[:, :, cells_lat - d :])
        sends = [([(k, k ^ 1) for k in range(2 * nlon_dev)], facing)]
    else:
        sends = [
            (pairs_from(0, -1), wide[:, :, cells_lat - d :]),
            (pairs_from(0, 1), wide[:, :, :d]),
        ]
    lat_sends = len(sends)
    while small and span < nlon_dev:
        sends += [(pairs_from(-span, 0), window), (pairs_from(span, 0), window)]
        got = exchange(sends)
        window = jnp.concatenate([got[-2], window, got[-1]], axis=1)
        span, sends = 3 * span, []
        if len(got) == lat_sends + 2:
            lat_got = got[:lat_sends]
    if sends:
        lat_got = exchange(sends)
    south, north = (lat_got[0], lat_got[0]) if lat_peers == 2 else lat_got

    if small:
        gathered, base = window, col0 - (span // 2) * cells_lon
    else:
        gathered, base = lax.all_gather(top, "lon", axis=1, tiled=True), 0
    pivot = fold_partner[0]
    first = (pivot - col0 - cells_lon - depth + 1 - base) % nlon
    doubled = jnp.concatenate([gathered[:, :nlon], gathered[:, :width]], axis=1)
    mirror = lax.dynamic_slice_in_dim(doubled, first, width, axis=1)[:, ::-1, ::-1]

    south_band, north_band = south, north
    north_band = jnp.where(is_top, mirror, north_band)
    ext = jnp.concatenate([south_band, wide, north_band], axis=2)

    mask = ext[nfield : nfield + nlev]
    kappa_e = ext[nfield + nlev]
    kappa_n = ext[nfield + nlev + 1]
    r = jnp.arange(rows, dtype=jnp.int32)
    virtual = (is_top & (r >= depth + cells_lat))[None, :]
    fold_row = (is_top & (r == depth + cells_lat - 1))[None, :]
    south_edge = (is_bottom & (r < depth))[None, :]
    kappa_e = jnp.where(virtual, jnp.roll(kappa_e, -1, axis=0), kappa_e)
    kappa_up = jnp.roll(kappa_n, -1, axis=1)
    kappa_n = jnp.where(
        virtual, kappa_up, jnp.where(fold_row, 0.5 * (kappa_n + kappa_up), kappa_n)
    )
    coef_e = kappa_e * mask * jnp.roll(mask, -1, axis=1)
    coef_n = kappa_n * mask * jnp.roll(mask, -1, axis=2)
    coef_n = jnp.where(south_edge[None], 0.0, coef_n)

    v = ext[:nfield].reshape(nvar, nlev, width, rows)
    for sweep in range(STEPS):
        flux_e = coef_e * (jnp.roll(v, -1, axis=2) - v)
        flux_n = coef_n * (jnp.roll(v, -1, axis=3) - v)
        v = v + (flux_e - jnp.roll(flux_e, 1, axis=2)) + (flux_n - jnp.roll(flux_n, 1, axis=3))
    own = v[:, :, depth : depth + cells_lon, depth : depth + cells_lat]
    return error_std * own


def solution(mesh):
    return jax.shard_map(
        per_device,
        mesh=mesh,
        in_specs=(
            P("ens", None, "lon", "lat"),
            P(None, None, "lon", "lat"),
            P(None, "lon", "lat"),
            P("lon", "lat"),
            P("lon", "lat"),
            P(),
        ),
        out_specs=P("ens", None, "lon", "lat"),
        check_vma=False,
    )
```

```python
import jax
import jax.numpy as jnp
from jax import lax
from jax.experimental import pallas as pl
from jax.experimental.pallas import tpu as pltpu
from jax.sharding import PartitionSpec as P

STEPS = 8


AXES = ("lon", "lat")


def exchange(sends):
    groups = {}
    for k, (pairs, x) in enumerate(sends):
        groups.setdefault(tuple(pairs), []).append(k)
    out = [None] * len(sends)
    for pairs, members in groups.items():
        if len(members) == 1:
            out[members[0]] = lax.ppermute(sends[members[0]][1], AXES, list(pairs))
            continue
        flat = jnp.concatenate([sends[k][1].reshape(-1) for k in members])
        got = lax.ppermute(flat, AXES, list(pairs))
        offset = 0
        for k in members:
            size = sends[k][1].size
            out[k] = got[offset : offset + size].reshape(sends[k][1].shape)
            offset += size
    return out


def pairs_from(d_lon, d_lat):
    nlon, nlat = lax.axis_size("lon"), lax.axis_size("lat")
    pairs = []
    for lon in range(nlon):
        for lat in range(nlat):
            dst = lat - d_lat
            if 0 <= dst < nlat:
                pairs.append((lon * nlat + lat, ((lon - d_lon) % nlon) * nlat + dst))
    return pairs


def per_device(control, error_std, land_mask, diff_east, diff_north, fold_partner):
    nvar, nlev, cells_lon, cells_lat = control.shape
    depth = STEPS
    nlon = fold_partner.shape[0]
    width = cells_lon + 2 * depth
    rows = cells_lat + 2 * depth
    nfield = nvar * nlev
    lat_index, lat_peers = lax.axis_index("lat"), lax.axis_size("lat")
    is_top = lat_index == lat_peers - 1
    is_bottom = lat_index == 0
    col0 = lax.axis_index("lon") * cells_lon

    field = (error_std * control).reshape(nfield, cells_lon, cells_lat)
    stack = jnp.concatenate(
        [field, land_mask.astype(jnp.float32), diff_east[None], diff_north[None]], axis=0
    )

    nlon_dev = lax.axis_size("lon")
    d = depth
    top = stack[:, :, cells_lat - d :]
    small = nlon_dev <= 16
    west, east, from_west, from_east = exchange(
        [
            (pairs_from(-1, 0), stack[:, cells_lon - d :]),
            (pairs_from(1, 0), stack[:, :d]),
            (pairs_from(-1, 0), top),
            (pairs_from(1, 0), top),
        ]
    )
    wide = jnp.concatenate([stack, east, west], axis=1)
    window, span = jnp.concatenate([from_west, top, from_east], axis=1), 3
    if lat_peers == 2:
        facing = jnp.where(is_top, wide[:, :, :d], wide[:, :, cells_lat - d :])
        sends = [([(k, k ^ 1) for k in range(2 * nlon_dev)], facing)]
    else:
        sends = [
            (pairs_from(0, -1), wide[:, :, cells_lat - d :]),
            (pairs_from(0, 1), wide[:, :, :d]),
        ]
    lat_sends = len(sends)
    while small and span < nlon_dev:
        sends += [(pairs_from(-span, 0), window), (pairs_from(span, 0), window)]
        got = exchange(sends)
        window = jnp.concatenate([got[-2], window, got[-1]], axis=1)
        span, sends = 3 * span, []
        if len(got) == lat_sends + 2:
            lat_got = got[:lat_sends]
    if sends:
        lat_got = exchange(sends)
    south, north = (lat_got[0], lat_got[0]) if lat_peers == 2 else lat_got

    if small:
        gathered, base = window, col0 - (span // 2) * cells_lon
    else:
        gathered, base = lax.all_gather(top, "lon", axis=1, tiled=True), 0
    pivot = fold_partner[0]
    first = (pivot - col0 - cells_lon - depth + 1 - base) % nlon
    doubled = jnp.concatenate([gathered[:, :nlon], gathered[:, :width]], axis=1)
    mirror = lax.dynamic_slice_in_dim(doubled, first, width, axis=1)[:, ::-1, ::-1]
    mirror = jnp.concatenate([mirror[:, d:], mirror[:, :d]], axis=1)
    north = jnp.where(is_top, mirror, north)

    lanes = -(-(cells_lat + 2 * d) // 128) * 128
    spare = jnp.zeros((stack.shape[0], width, lanes - cells_lat - 2 * d), jnp.float32)
    ext = jnp.concatenate([wide, north, spare, south], axis=2)
    flags = jnp.stack([is_top, is_bottom]).astype(jnp.int32)
    out = pl.pallas_call(
        lambda *refs: diffuse_kernel(*refs, nvar=nvar, nlev=nlev, cells=(cells_lon, cells_lat), depth=d),
        out_shape=jax.ShapeDtypeStruct((nfield, cells_lon, cells_lat), jnp.float32),
        in_specs=[
            pl.BlockSpec(memory_space=pltpu.SMEM),
            pl.BlockSpec(memory_space=pltpu.VMEM),
            pl.BlockSpec(memory_space=pltpu.VMEM),
        ],
        out_specs=pl.BlockSpec(memory_space=pltpu.VMEM),
    )(flags, ext, error_std.reshape(nfield, cells_lon, cells_lat))
    return out.reshape(control.shape)


def diffuse_kernel(flags_ref, ext_ref, std_ref, out_ref, *, nvar, nlev, cells, depth):
    cells_lon, cells_lat = cells
    nfield = nvar * nlev
    width, lanes = ext_ref.shape[1], ext_ref.shape[2]
    is_top = flags_ref[0] == 1
    is_bottom = flags_ref[1] == 1

    def next_col(x):
        return pltpu.roll(x, width - 1, 0)

    def next_row(x):
        return pltpu.roll(x, lanes - 1, 1)

    row = lax.broadcasted_iota(jnp.int32, (width, lanes), 1)
    virtual = is_top & (row >= cells_lat) & (row < cells_lat + depth)
    fold_row = is_top & (row == cells_lat - 1)
    south_edge = is_bottom & (row == lanes - 1)
    kappa_e = ext_ref[nfield + nlev]
    kappa_n = ext_ref[nfield + nlev + 1]
    kappa_e = jnp.where(virtual, next_col(kappa_e), kappa_e)
    kappa_up = next_row(kappa_n)
    kappa_n = jnp.where(virtual, kappa_up, jnp.where(fold_row, 0.5 * (kappa_n + kappa_up), kappa_n))
    for lev in range(nlev):
        mask = ext_ref[nfield + lev]
        coef_e = kappa_e * mask * next_col(mask)
        coef_n = jnp.where(south_edge, 0.0, kappa_n * mask * next_row(mask))
        for var in range(nvar):
            plane = var * nlev + lev
            v = ext_ref[plane]
            for sweep in range(STEPS):
                flux_e = coef_e * (next_col(v) - v)
                flux_n = coef_n * (next_row(v) - v)
                v = v + (flux_e - pltpu.roll(flux_e, 1, 0)) + (flux_n - pltpu.roll(flux_n, 1, 1))
            out_ref[plane] = std_ref[plane] * v[:cells_lon, :cells_lat]


def solution(mesh):
    return jax.shard_map(
        per_device,
        mesh=mesh,
        in_specs=(
            P("ens", None, "lon", "lat"),
            P(None, None, "lon", "lat"),
            P(None, "lon", "lat"),
            P("lon", "lat"),
            P("lon", "lat"),
            P(),
        ),
        out_specs=P("ens", None, "lon", "lat"),
        check_vma=False,
    )
```

```python
import jax
import jax.numpy as jnp
from jax import lax
from jax.experimental import pallas as pl
from jax.experimental.pallas import tpu as pltpu
from jax.sharding import PartitionSpec as P

STEPS = 8


AXES = ("lon", "lat")


def exchange(sends):
    groups = {}
    for k, (pairs, x) in enumerate(sends):
        groups.setdefault(tuple(pairs), []).append(k)
    out = [None] * len(sends)
    for pairs, members in groups.items():
        if len(members) == 1:
            out[members[0]] = lax.ppermute(sends[members[0]][1], AXES, list(pairs))
            continue
        flat = jnp.concatenate([sends[k][1].reshape(-1) for k in members])
        got = lax.ppermute(flat, AXES, list(pairs))
        offset = 0
        for k in members:
            size = sends[k][1].size
            out[k] = got[offset : offset + size].reshape(sends[k][1].shape)
            offset += size
    return out


def pairs_from(d_lon, d_lat, lats=None):
    nlon, nlat = lax.axis_size("lon"), lax.axis_size("lat")
    pairs = []
    for lon in range(nlon):
        for lat in range(nlat) if lats is None else lats:
            dst = lat - d_lat
            if 0 <= dst < nlat:
                pairs.append((lon * nlat + lat, ((lon - d_lon) % nlon) * nlat + dst))
    return pairs


def per_device(control, error_std, land_mask, diff_east, diff_north, fold_partner):
    nvar, nlev, cells_lon, cells_lat = control.shape
    depth = STEPS
    nlon = fold_partner.shape[0]
    width = cells_lon + 2 * depth
    rows = cells_lat + 2 * depth
    nfield = nvar * nlev
    lat_index, lat_peers = lax.axis_index("lat"), lax.axis_size("lat")
    is_top = lat_index == lat_peers - 1
    is_bottom = lat_index == 0
    col0 = lax.axis_index("lon") * cells_lon

    field = (error_std * control).reshape(nfield, cells_lon, cells_lat)
    stack = jnp.concatenate(
        [field, land_mask.astype(jnp.float32), diff_east[None], diff_north[None]], axis=0
    )

    nlon_dev = lax.axis_size("lon")
    d = depth
    top = stack[:, :, cells_lat - d :]
    small = nlon_dev <= 16
    west, east, from_west, from_east = exchange(
        [
            (pairs_from(-1, 0), stack[:, cells_lon - d :]),
            (pairs_from(1, 0), stack[:, :d]),
            (pairs_from(-1, 0), top),
            (pairs_from(1, 0), top),
        ]
    )
    wide = jnp.concatenate([stack, east, west], axis=1)
    window, span = jnp.concatenate([from_west, top, from_east], axis=1), 3
    if lat_peers == 2:
        facing = jnp.where(is_top, wide[:, :, :d], wide[:, :, cells_lat - d :])
        sends = [([(k, k ^ 1) for k in range(2 * nlon_dev)], facing)]
    else:
        sends = [
            (pairs_from(0, -1), wide[:, :, cells_lat - d :]),
            (pairs_from(0, 1), wide[:, :, :d]),
        ]
    lat_sends = len(sends)
    while small and span < nlon_dev:
        tops = [lat_peers - 1]
        sends += [(pairs_from(-span, 0, tops), window), (pairs_from(span, 0, tops), window)]
        got = exchange(sends)
        window = jnp.concatenate([got[-2], window, got[-1]], axis=1)
        span, sends = 3 * span, []
        if len(got) == lat_sends + 2:
            lat_got = got[:lat_sends]
    if sends:
        lat_got = exchange(sends)
    south, north = (lat_got[0], lat_got[0]) if lat_peers == 2 else lat_got

    if small:
        gathered, base = window, col0 - (span // 2) * cells_lon
    else:
        gathered, base = lax.all_gather(top, "lon", axis=1, tiled=True), 0
    pivot = fold_partner[0]
    first = (pivot - col0 - cells_lon - depth + 1 - base) % nlon
    doubled = jnp.concatenate([gathered[:, :nlon], gathered[:, :width]], axis=1)
    mirror = lax.dynamic_slice_in_dim(doubled, first, width, axis=1)[:, ::-1, ::-1]
    mirror = jnp.concatenate([mirror[:, d:], mirror[:, :d]], axis=1)
    north = jnp.where(is_top, mirror, north)

    lanes = -(-(cells_lat + 2 * d) // 128) * 128
    flags = jnp.stack([is_top, is_bottom]).astype(jnp.int32)
    vmem = pl.BlockSpec(memory_space=pltpu.VMEM)
    out = pl.pallas_call(
        lambda *refs: diffuse_kernel(*refs, nvar=nvar, nlev=nlev, depth=d),
        out_shape=jax.ShapeDtypeStruct((nfield, cells_lon, cells_lat), jnp.float32),
        in_specs=[pl.BlockSpec(memory_space=pltpu.SMEM)] + [vmem] * 6,
        out_specs=vmem,
        scratch_shapes=[pltpu.VMEM((stack.shape[0], width, lanes), jnp.float32)],
    )(flags, stack, east, west, north, south, error_std.reshape(nfield, cells_lon, cells_lat))
    return out.reshape(control.shape)


def diffuse_kernel(
    flags_ref, own_ref, east_ref, west_ref, north_ref, south_ref, std_ref, out_ref, ext_ref,
    *, nvar, nlev, depth
):
    nfield = nvar * nlev
    cells_lon, cells_lat = own_ref.shape[1:]
    width, lanes = ext_ref.shape[1], ext_ref.shape[2]
    is_top = flags_ref[0] == 1
    is_bottom = flags_ref[1] == 1
    ext_ref[:, :, cells_lat:] = jnp.zeros((ext_ref.shape[0], width, lanes - cells_lat), jnp.float32)
    ext_ref[:, :cells_lon, :cells_lat] = own_ref[...]
    ext_ref[:, cells_lon : cells_lon + depth, :cells_lat] = east_ref[...]
    ext_ref[:, cells_lon + depth :, :cells_lat] = west_ref[...]
    ext_ref[:, :, cells_lat : cells_lat + depth] = north_ref[...]
    ext_ref[:, :, lanes - depth :] = south_ref[...]

    def next_col(x):
        return pltpu.roll(x, width - 1, 0)

    def next_row(x):
        return pltpu.roll(x, lanes - 1, 1)

    row = lax.broadcasted_iota(jnp.int32, (width, lanes), 1)
    virtual = is_top & (row >= cells_lat) & (row < cells_lat + depth)
    fold_row = is_top & (row == cells_lat - 1)
    south_edge = is_bottom & (row == lanes - 1)
    kappa_e = ext_ref[nfield + nlev]
    kappa_n = ext_ref[nfield + nlev + 1]
    kappa_e = jnp.where(virtual, next_col(kappa_e), kappa_e)
    kappa_up = next_row(kappa_n)
    kappa_n = jnp.where(virtual, kappa_up, jnp.where(fold_row, 0.5 * (kappa_n + kappa_up), kappa_n))
    for lev in range(nlev):
        mask = ext_ref[nfield + lev]
        coef_e = kappa_e * mask * next_col(mask)
        coef_n = jnp.where(south_edge, 0.0, kappa_n * mask * next_row(mask))
        for var in range(nvar):
            plane = var * nlev + lev
            v = ext_ref[plane]
            for sweep in range(STEPS):
                flux_e = coef_e * (next_col(v) - v)
                flux_n = coef_n * (next_row(v) - v)
                v = v + (flux_e - pltpu.roll(flux_e, 1, 0)) + (flux_n - pltpu.roll(flux_n, 1, 1))
            out_ref[plane] = std_ref[plane] * v[:cells_lon, :cells_lat]


def solution(mesh):
    return jax.shard_map(
        per_device,
        mesh=mesh,
        in_specs=(
            P("ens", None, "lon", "lat"),
            P(None, None, "lon", "lat"),
            P(None, "lon", "lat"),
            P("lon", "lat"),
            P("lon", "lat"),
            P(),
        ),
        out_specs=P("ens", None, "lon", "lat"),
        check_vma=False,
    )
```

```python
import jax
import jax.numpy as jnp
from jax import lax
from jax.experimental import pallas as pl
from jax.experimental.pallas import tpu as pltpu
from jax.sharding import PartitionSpec as P

STEPS = 8


AXES = ("lon", "lat")


def exchange(sends):
    groups = {}
    for k, (pairs, x) in enumerate(sends):
        groups.setdefault(tuple(pairs), []).append(k)
    out = [None] * len(sends)
    for pairs, members in groups.items():
        if len(members) == 1:
            out[members[0]] = lax.ppermute(sends[members[0]][1], AXES, list(pairs))
            continue
        flat = jnp.concatenate([sends[k][1].reshape(-1) for k in members])
        got = lax.ppermute(flat, AXES, list(pairs))
        offset = 0
        for k in members:
            size = sends[k][1].size
            out[k] = got[offset : offset + size].reshape(sends[k][1].shape)
            offset += size
    return out


def pairs_from(d_lon, d_lat, lats=None):
    nlon, nlat = lax.axis_size("lon"), lax.axis_size("lat")
    pairs = []
    for lon in range(nlon):
        for lat in range(nlat) if lats is None else lats:
            dst = lat - d_lat
            if 0 <= dst < nlat:
                pairs.append((lon * nlat + lat, ((lon - d_lon) % nlon) * nlat + dst))
    return pairs


def per_device(control, error_std, land_mask, diff_east, diff_north, fold_partner):
    nvar, nlev, cells_lon, cells_lat = control.shape
    depth = STEPS
    nlon = fold_partner.shape[0]
    width = cells_lon + 2 * depth
    rows = cells_lat + 2 * depth
    nfield = nvar * nlev
    lat_index, lat_peers = lax.axis_index("lat"), lax.axis_size("lat")
    is_top = lat_index == lat_peers - 1
    is_bottom = lat_index == 0
    col0 = lax.axis_index("lon") * cells_lon

    field = (error_std * control).reshape(nfield, cells_lon, cells_lat)
    stack = jnp.concatenate(
        [field, land_mask.astype(jnp.float32), diff_east[None], diff_north[None]], axis=0
    )

    nlon_dev = lax.axis_size("lon")
    d = depth
    top = stack[:, :, cells_lat - d :]
    small = nlon_dev <= 16
    west, east = exchange(
        [(pairs_from(-1, 0), stack[:, cells_lon - d :]), (pairs_from(1, 0), stack[:, :d])]
    )
    wide = jnp.concatenate([stack, east, west], axis=1)
    if lat_peers == 2:
        facing = jnp.where(is_top, wide[:, :, :d], wide[:, :, cells_lat - d :])
        sends = [([(k, k ^ 1) for k in range(2 * nlon_dev)], facing)]
    else:
        sends = [
            (pairs_from(0, -1), wide[:, :, cells_lat - d :]),
            (pairs_from(0, 1), wide[:, :, :d]),
        ]
    lat_got = exchange(sends)
    south, north = (lat_got[0], lat_got[0]) if lat_peers == 2 else lat_got

    if small:
        copies = jnp.broadcast_to(top[None], (nlon_dev,) + top.shape)
        strips = lax.all_to_all(copies, "lon", 0, 0)
        gathered = jnp.concatenate([strips[k] for k in range(nlon_dev)], axis=1)
    else:
        gathered = lax.all_gather(top, "lon", axis=1, tiled=True)
    base = 0
    pivot = fold_partner[0]
    first = (pivot - col0 - cells_lon - depth + 1 - base) % nlon
    doubled = jnp.concatenate([gathered[:, :nlon], gathered[:, :width]], axis=1)
    mirror = lax.dynamic_slice_in_dim(doubled, first, width, axis=1)[:, ::-1, ::-1]
    mirror = jnp.concatenate([mirror[:, d:], mirror[:, :d]], axis=1)
    north = jnp.where(is_top, mirror, north)

    lanes = -(-(cells_lat + 2 * d) // 128) * 128
    flags = jnp.stack([is_top, is_bottom]).astype(jnp.int32)
    vmem = pl.BlockSpec(memory_space=pltpu.VMEM)
    out = pl.pallas_call(
        lambda *refs: diffuse_kernel(*refs, nvar=nvar, nlev=nlev, depth=d),
        out_shape=jax.ShapeDtypeStruct((nfield, cells_lon, cells_lat), jnp.float32),
        in_specs=[pl.BlockSpec(memory_space=pltpu.SMEM)] + [vmem] * 6,
        out_specs=vmem,
        scratch_shapes=[pltpu.VMEM((stack.shape[0], width, lanes), jnp.float32)],
    )(flags, stack, east, west, north, south, error_std.reshape(nfield, cells_lon, cells_lat))
    return out.reshape(control.shape)


def diffuse_kernel(
    flags_ref, own_ref, east_ref, west_ref, north_ref, south_ref, std_ref, out_ref, ext_ref,
    *, nvar, nlev, depth
):
    nfield = nvar * nlev
    cells_lon, cells_lat = own_ref.shape[1:]
    width, lanes = ext_ref.shape[1], ext_ref.shape[2]
    is_top = flags_ref[0] == 1
    is_bottom = flags_ref[1] == 1
    ext_ref[:, :, cells_lat:] = jnp.zeros((ext_ref.shape[0], width, lanes - cells_lat), jnp.float32)
    ext_ref[:, :cells_lon, :cells_lat] = own_ref[...]
    ext_ref[:, cells_lon : cells_lon + depth, :cells_lat] = east_ref[...]
    ext_ref[:, cells_lon + depth :, :cells_lat] = west_ref[...]
    ext_ref[:, :, cells_lat : cells_lat + depth] = north_ref[...]
    ext_ref[:, :, lanes - depth :] = south_ref[...]

    def next_col(x):
        return pltpu.roll(x, width - 1, 0)

    def next_row(x):
        return pltpu.roll(x, lanes - 1, 1)

    row = lax.broadcasted_iota(jnp.int32, (width, lanes), 1)
    virtual = is_top & (row >= cells_lat) & (row < cells_lat + depth)
    fold_row = is_top & (row == cells_lat - 1)
    south_edge = is_bottom & (row == lanes - 1)
    kappa_e = ext_ref[nfield + nlev]
    kappa_n = ext_ref[nfield + nlev + 1]
    kappa_e = jnp.where(virtual, next_col(kappa_e), kappa_e)
    kappa_up = next_row(kappa_n)
    kappa_n = jnp.where(virtual, kappa_up, jnp.where(fold_row, 0.5 * (kappa_n + kappa_up), kappa_n))
    for lev in range(nlev):
        mask = ext_ref[nfield + lev]
        coef_e = kappa_e * mask * next_col(mask)
        coef_n = jnp.where(south_edge, 0.0, kappa_n * mask * next_row(mask))
        for var in range(nvar):
            plane = var * nlev + lev
            v = ext_ref[plane]
            for sweep in range(STEPS):
                flux_e = coef_e * (next_col(v) - v)
                flux_n = coef_n * (next_row(v) - v)
                v = v + (flux_e - pltpu.roll(flux_e, 1, 0)) + (flux_n - pltpu.roll(flux_n, 1, 1))
            out_ref[plane] = std_ref[plane] * v[:cells_lon, :cells_lat]


def solution(mesh):
    return jax.shard_map(
        per_device,
        mesh=mesh,
        in_specs=(
            P("ens", None, "lon", "lat"),
            P(None, None, "lon", "lat"),
            P(None, "lon", "lat"),
            P("lon", "lat"),
            P("lon", "lat"),
            P(),
        ),
        out_specs=P("ens", None, "lon", "lat"),
        check_vma=False,
    )
```

```python
import jax
import jax.numpy as jnp
from jax import lax
from jax.experimental import pallas as pl
from jax.experimental.pallas import tpu as pltpu
from jax.sharding import PartitionSpec as P

STEPS = 8


AXES = ("lon", "lat")


def exchange(sends):
    groups = {}
    for k, (pairs, x) in enumerate(sends):
        groups.setdefault(tuple(pairs), []).append(k)
    out = [None] * len(sends)
    for pairs, members in groups.items():
        if len(members) == 1:
            out[members[0]] = lax.ppermute(sends[members[0]][1], AXES, list(pairs))
            continue
        flat = jnp.concatenate([sends[k][1].reshape(-1) for k in members])
        got = lax.ppermute(flat, AXES, list(pairs))
        offset = 0
        for k in members:
            size = sends[k][1].size
            out[k] = got[offset : offset + size].reshape(sends[k][1].shape)
            offset += size
    return out


def pairs_from(d_lon, d_lat, lats=None):
    nlon, nlat = lax.axis_size("lon"), lax.axis_size("lat")
    pairs = []
    for lon in range(nlon):
        for lat in range(nlat) if lats is None else lats:
            dst = lat - d_lat
            if 0 <= dst < nlat:
                pairs.append((lon * nlat + lat, ((lon - d_lon) % nlon) * nlat + dst))
    return pairs


def per_device(control, error_std, land_mask, diff_east, diff_north, fold_partner):
    nvar, nlev, cells_lon, cells_lat = control.shape
    depth = STEPS
    nlon = fold_partner.shape[0]
    width = cells_lon + 2 * depth
    rows = cells_lat + 2 * depth
    nfield = nvar * nlev
    lat_index, lat_peers = lax.axis_index("lat"), lax.axis_size("lat")
    is_top = lat_index == lat_peers - 1
    is_bottom = lat_index == 0
    col0 = lax.axis_index("lon") * cells_lon

    field = (error_std * control).reshape(nfield, cells_lon, cells_lat)
    stack = jnp.concatenate(
        [field, land_mask.astype(jnp.float32), diff_east[None], diff_north[None]], axis=0
    )

    nlon_dev = lax.axis_size("lon")
    d = depth
    top = stack[:, :, cells_lat - d :]
    small = nlon_dev <= 16
    west, east = exchange(
        [(pairs_from(-1, 0), stack[:, cells_lon - d :]), (pairs_from(1, 0), stack[:, :d])]
    )
    wide = jnp.concatenate([stack, east, west], axis=1)
    if lat_peers == 2:
        facing = jnp.where(is_top, wide[:, :, :d], wide[:, :, cells_lat - d :])
        sends = [([(k, k ^ 1) for k in range(2 * nlon_dev)], facing)]
    else:
        sends = [
            (pairs_from(0, -1), wide[:, :, cells_lat - d :]),
            (pairs_from(0, 1), wide[:, :, :d]),
        ]
    lat_got = exchange(sends)
    south, north = (lat_got[0], lat_got[0]) if lat_peers == 2 else lat_got

    if small:
        flipped = top[:, ::-1, ::-1].reshape(1, -1)
        copies = jnp.broadcast_to(flipped, (nlon_dev, flipped.shape[1]))
        strips = lax.all_to_all(copies, "lon", 0, 0)
        ring = jnp.concatenate(
            [strips[k].reshape(top.shape) for k in range(nlon_dev - 1, -1, -1)], axis=1
        )
    else:
        ring = lax.all_gather(top, "lon", axis=1, tiled=True)[:, ::-1, ::-1]
    pivot = fold_partner[0]
    first = (col0 - depth - pivot - 1) % nlon
    doubled = jnp.concatenate([ring, ring[:, :width]], axis=1)
    mirror = lax.dynamic_slice_in_dim(doubled, first, width, axis=1)
    mirror = jnp.concatenate([mirror[:, d:], mirror[:, :d]], axis=1)

    lanes = -(-(cells_lat + 2 * d) // 128) * 128
    flags = jnp.stack([is_top, is_bottom]).astype(jnp.int32)
    vmem = pl.BlockSpec(memory_space=pltpu.VMEM)
    out = pl.pallas_call(
        lambda *refs: diffuse_kernel(*refs, nvar=nvar, nlev=nlev, depth=d),
        out_shape=jax.ShapeDtypeStruct((nfield, cells_lon, cells_lat), jnp.float32),
        in_specs=[pl.BlockSpec(memory_space=pltpu.SMEM)] + [vmem] * 7,
        out_specs=vmem,
        scratch_shapes=[pltpu.VMEM((stack.shape[0], width, lanes), jnp.float32)],
    )(flags, stack, east, west, north, mirror, south, error_std.reshape(nfield, cells_lon, cells_lat))
    return out.reshape(control.shape)


def diffuse_kernel(
    flags_ref, own_ref, east_ref, west_ref, north_ref, mirror_ref, south_ref, std_ref, out_ref, ext_ref,
    *, nvar, nlev, depth
):
    nfield = nvar * nlev
    cells_lon, cells_lat = own_ref.shape[1:]
    width, lanes = ext_ref.shape[1], ext_ref.shape[2]
    is_top = flags_ref[0] == 1
    is_bottom = flags_ref[1] == 1
    ext_ref[:, :, cells_lat:] = jnp.zeros((ext_ref.shape[0], width, lanes - cells_lat), jnp.float32)
    ext_ref[:, :cells_lon, :cells_lat] = own_ref[...]
    ext_ref[:, cells_lon : cells_lon + depth, :cells_lat] = east_ref[...]
    ext_ref[:, cells_lon + depth :, :cells_lat] = west_ref[...]
    ext_ref[:, :, cells_lat : cells_lat + depth] = jnp.where(is_top, mirror_ref[...], north_ref[...])
    ext_ref[:, :, lanes - depth :] = south_ref[...]

    def next_col(x):
        return pltpu.roll(x, width - 1, 0)

    def next_row(x):
        return pltpu.roll(x, lanes - 1, 1)

    row = lax.broadcasted_iota(jnp.int32, (width, lanes), 1)
    virtual = is_top & (row >= cells_lat) & (row < cells_lat + depth)
    fold_row = is_top & (row == cells_lat - 1)
    south_edge = is_bottom & (row == lanes - 1)
    kappa_e = ext_ref[nfield + nlev]
    kappa_n = ext_ref[nfield + nlev + 1]
    kappa_e = jnp.where(virtual, next_col(kappa_e), kappa_e)
    kappa_up = next_row(kappa_n)
    kappa_n = jnp.where(virtual, kappa_up, jnp.where(fold_row, 0.5 * (kappa_n + kappa_up), kappa_n))
    for lev in range(nlev):
        mask = ext_ref[nfield + lev]
        coef_e = kappa_e * mask * next_col(mask)
        coef_n = jnp.where(south_edge, 0.0, kappa_n * mask * next_row(mask))
        for var in range(nvar):
            plane = var * nlev + lev
            v = ext_ref[plane]
            for sweep in range(STEPS):
                flux_e = coef_e * (next_col(v) - v)
                flux_n = coef_n * (next_row(v) - v)
                v = v + (flux_e - pltpu.roll(flux_e, 1, 0)) + (flux_n - pltpu.roll(flux_n, 1, 1))
            out_ref[plane] = std_ref[plane] * v[:cells_lon, :cells_lat]


def solution(mesh):
    return jax.shard_map(
        per_device,
        mesh=mesh,
        in_specs=(
            P("ens", None, "lon", "lat"),
            P(None, None, "lon", "lat"),
            P(None, "lon", "lat"),
            P("lon", "lat"),
            P("lon", "lat"),
            P(),
        ),
        out_specs=P("ens", None, "lon", "lat"),
        check_vma=False,
    )
```

```python
import jax
import jax.numpy as jnp
from jax import lax
from jax.experimental import pallas as pl
from jax.experimental.pallas import tpu as pltpu
from jax.sharding import PartitionSpec as P

STEPS = 8


AXES = ("lon", "lat")


def exchange(sends):
    groups = {}
    for k, (pairs, x) in enumerate(sends):
        groups.setdefault(tuple(pairs), []).append(k)
    out = [None] * len(sends)
    for pairs, members in groups.items():
        if len(members) == 1:
            out[members[0]] = lax.ppermute(sends[members[0]][1], AXES, list(pairs))
            continue
        flat = jnp.concatenate([sends[k][1].reshape(-1) for k in members])
        got = lax.ppermute(flat, AXES, list(pairs))
        offset = 0
        for k in members:
            size = sends[k][1].size
            out[k] = got[offset : offset + size].reshape(sends[k][1].shape)
            offset += size
    return out


def pairs_from(d_lon, d_lat, lats=None):
    nlon, nlat = lax.axis_size("lon"), lax.axis_size("lat")
    pairs = []
    for lon in range(nlon):
        for lat in range(nlat) if lats is None else lats:
            dst = lat - d_lat
            if 0 <= dst < nlat:
                pairs.append((lon * nlat + lat, ((lon - d_lon) % nlon) * nlat + dst))
    return pairs


def per_device(control, error_std, land_mask, diff_east, diff_north, fold_partner):
    nvar, nlev, cells_lon, cells_lat = control.shape
    depth = STEPS
    nlon = fold_partner.shape[0]
    width = cells_lon + 2 * depth
    rows = cells_lat + 2 * depth
    nfield = nvar * nlev
    lat_index, lat_peers = lax.axis_index("lat"), lax.axis_size("lat")
    is_top = lat_index == lat_peers - 1
    is_bottom = lat_index == 0
    col0 = lax.axis_index("lon") * cells_lon

    def planes(cols, rows):
        field = error_std[:, :, cols, rows] * control[:, :, cols, rows]
        return jnp.concatenate(
            [
                field.reshape((nfield,) + field.shape[2:]),
                land_mask[:, cols, rows].astype(jnp.float32),
                diff_east[None, cols, rows],
                diff_north[None, cols, rows],
            ],
            axis=0,
        )

    every = slice(None)

    nlon_dev = lax.axis_size("lon")
    d = depth
    top = planes(every, slice(cells_lat - d, None))
    small = nlon_dev <= 16
    west, east = exchange(
        [
            (pairs_from(-1, 0), planes(slice(cells_lon - d, None), every)),
            (pairs_from(1, 0), planes(slice(0, d), every)),
        ]
    )
    def wide_rows(rows):
        return jnp.concatenate([planes(every, rows), east[:, :, rows], west[:, :, rows]], axis=1)

    if lat_peers == 2:
        facing = jnp.where(is_top, wide_rows(slice(0, d)), wide_rows(slice(cells_lat - d, None)))
        sends = [([(k, k ^ 1) for k in range(2 * nlon_dev)], facing)]
    else:
        sends = [
            (pairs_from(0, -1), wide_rows(slice(cells_lat - d, None))),
            (pairs_from(0, 1), wide_rows(slice(0, d))),
        ]
    lat_got = exchange(sends)
    south, north = (lat_got[0], lat_got[0]) if lat_peers == 2 else lat_got

    if small:
        copies = jnp.broadcast_to(top[None], (nlon_dev,) + top.shape)
        strips = lax.all_to_all(copies, "lon", 0, 0)
        gathered = jnp.concatenate([strips[k] for k in range(nlon_dev)], axis=1)
    else:
        gathered = lax.all_gather(top, "lon", axis=1, tiled=True)
    base = 0
    pivot = fold_partner[0]
    first = (pivot - col0 - cells_lon - depth + 1 - base) % nlon
    doubled = jnp.concatenate([gathered[:, :nlon], gathered[:, :width]], axis=1)
    mirror = lax.dynamic_slice_in_dim(doubled, first, width, axis=1)[:, ::-1, ::-1]
    mirror = jnp.concatenate([mirror[:, d:], mirror[:, :d]], axis=1)
    north = jnp.where(is_top, mirror, north)

    lanes = -(-(cells_lat + 2 * d) // 128) * 128
    flags = jnp.stack([is_top, is_bottom]).astype(jnp.int32)
    vmem = pl.BlockSpec(memory_space=pltpu.VMEM)
    out = pl.pallas_call(
        lambda *refs: diffuse_kernel(*refs, nvar=nvar, nlev=nlev, depth=d),
        out_shape=jax.ShapeDtypeStruct((nfield, cells_lon, cells_lat), jnp.float32),
        in_specs=[pl.BlockSpec(memory_space=pltpu.SMEM)] + [vmem] * 9,
        out_specs=vmem,
        scratch_shapes=[pltpu.VMEM((top.shape[0], width, lanes), jnp.float32)],
    )(
        flags,
        control.reshape(nfield, cells_lon, cells_lat),
        error_std.reshape(nfield, cells_lon, cells_lat),
        land_mask,
        diff_east,
        diff_north,
        east,
        west,
        north,
        south,
    )
    return out.reshape(control.shape)


def diffuse_kernel(
    flags_ref, control_ref, std_ref, mask_ref, kappa_e_ref, kappa_n_ref,
    east_ref, west_ref, north_ref, south_ref, out_ref, ext_ref, *, nvar, nlev, depth
):
    nfield = nvar * nlev
    cells_lon, cells_lat = control_ref.shape[1:]
    width, lanes = ext_ref.shape[1], ext_ref.shape[2]
    is_top = flags_ref[0] == 1
    is_bottom = flags_ref[1] == 1
    ext_ref[:, :, cells_lat:] = jnp.zeros((ext_ref.shape[0], width, lanes - cells_lat), jnp.float32)
    ext_ref[:nfield, :cells_lon, :cells_lat] = std_ref[...] * control_ref[...]
    ext_ref[nfield : nfield + nlev, :cells_lon, :cells_lat] = mask_ref[...].astype(jnp.float32)
    ext_ref[nfield + nlev, :cells_lon, :cells_lat] = kappa_e_ref[...]
    ext_ref[nfield + nlev + 1, :cells_lon, :cells_lat] = kappa_n_ref[...]
    ext_ref[:, cells_lon : cells_lon + depth, :cells_lat] = east_ref[...]
    ext_ref[:, cells_lon + depth :, :cells_lat] = west_ref[...]
    ext_ref[:, :, cells_lat : cells_lat + depth] = north_ref[...]
    ext_ref[:, :, lanes - depth :] = south_ref[...]

    def next_col(x):
        return pltpu.roll(x, width - 1, 0)

    def next_row(x):
        return pltpu.roll(x, lanes - 1, 1)

    row = lax.broadcasted_iota(jnp.int32, (width, lanes), 1)
    virtual = is_top & (row >= cells_lat) & (row < cells_lat + depth)
    fold_row = is_top & (row == cells_lat - 1)
    south_edge = is_bottom & (row == lanes - 1)
    kappa_e = ext_ref[nfield + nlev]
    kappa_n = ext_ref[nfield + nlev + 1]
    kappa_e = jnp.where(virtual, next_col(kappa_e), kappa_e)
    kappa_up = next_row(kappa_n)
    kappa_n = jnp.where(virtual, kappa_up, jnp.where(fold_row, 0.5 * (kappa_n + kappa_up), kappa_n))
    for lev in range(nlev):
        mask = ext_ref[nfield + lev]
        coef_e = kappa_e * mask * next_col(mask)
        coef_n = jnp.where(south_edge, 0.0, kappa_n * mask * next_row(mask))
        for var in range(nvar):
            plane = var * nlev + lev
            v = ext_ref[plane]
            for sweep in range(STEPS):
                flux_e = coef_e * (next_col(v) - v)
                flux_n = coef_n * (next_row(v) - v)
                v = v + (flux_e - pltpu.roll(flux_e, 1, 0)) + (flux_n - pltpu.roll(flux_n, 1, 1))
            out_ref[plane] = std_ref[plane] * v[:cells_lon, :cells_lat]


def solution(mesh):
    return jax.shard_map(
        per_device,
        mesh=mesh,
        in_specs=(
            P("ens", None, "lon", "lat"),
            P(None, None, "lon", "lat"),
            P(None, "lon", "lat"),
            P("lon", "lat"),
            P("lon", "lat"),
            P(),
        ),
        out_specs=P("ens", None, "lon", "lat"),
        check_vma=False,
    )
```

```python
import jax
import jax.numpy as jnp
from jax import lax
from jax.experimental import pallas as pl
from jax.experimental.pallas import tpu as pltpu
from jax.sharding import PartitionSpec as P

STEPS = 8


AXES = ("lon", "lat")


def exchange(sends):
    groups = {}
    for k, (pairs, x) in enumerate(sends):
        groups.setdefault(tuple(pairs), []).append(k)
    out = [None] * len(sends)
    for pairs, members in groups.items():
        if len(members) == 1:
            out[members[0]] = lax.ppermute(sends[members[0]][1], AXES, list(pairs))
            continue
        flat = jnp.concatenate([sends[k][1].reshape(-1) for k in members])
        got = lax.ppermute(flat, AXES, list(pairs))
        offset = 0
        for k in members:
            size = sends[k][1].size
            out[k] = got[offset : offset + size].reshape(sends[k][1].shape)
            offset += size
    return out


def pairs_from(d_lon, d_lat, lats=None):
    nlon, nlat = lax.axis_size("lon"), lax.axis_size("lat")
    pairs = []
    for lon in range(nlon):
        for lat in range(nlat) if lats is None else lats:
            dst = lat - d_lat
            if 0 <= dst < nlat:
                pairs.append((lon * nlat + lat, ((lon - d_lon) % nlon) * nlat + dst))
    return pairs


def per_device(control, error_std, land_mask, diff_east, diff_north, fold_partner):
    nvar, nlev, cells_lon, cells_lat = control.shape
    depth = STEPS
    nlon = fold_partner.shape[0]
    width = cells_lon + 2 * depth
    rows = cells_lat + 2 * depth
    nfield = nvar * nlev
    lat_index, lat_peers = lax.axis_index("lat"), lax.axis_size("lat")
    is_top = lat_index == lat_peers - 1
    is_bottom = lat_index == 0
    col0 = lax.axis_index("lon") * cells_lon

    field = (error_std * control).reshape(nfield, cells_lon, cells_lat)
    stack = jnp.concatenate(
        [field, land_mask.astype(jnp.float32), diff_east[None], diff_north[None]], axis=0
    )

    nlon_dev = lax.axis_size("lon")
    d = depth
    top = stack[:, :, cells_lat - d :]
    small = nlon_dev <= 16
    if 3 <= nlon_dev <= 16:
        lon_index = lax.axis_index("lon")
        halo_shape = (stack.shape[0], d, cells_lat)
        halo_size = stack.shape[0] * d * cells_lat
        strip = top.reshape(1, -1)
        dest = lax.broadcasted_iota(jnp.int32, (nlon_dev, 1), 0)
        right = stack[:, cells_lon - d :].reshape(1, -1)
        left = stack[:, :d].reshape(1, -1)
        halos = jnp.where(
            dest == (lon_index + 1) % nlon_dev,
            right,
            jnp.where(dest == (lon_index - 1) % nlon_dev, left, 0.0),
        )
        sent = jnp.concatenate([halos, jnp.broadcast_to(strip, (nlon_dev, strip.shape[1]))], axis=1)
        got = lax.all_to_all(sent, "lon", 0, 0)
        west = lax.dynamic_index_in_dim(got, (lon_index - 1) % nlon_dev, 0, False)
        east = lax.dynamic_index_in_dim(got, (lon_index + 1) % nlon_dev, 0, False)
        west = west[:halo_size].reshape(halo_shape)
        east = east[:halo_size].reshape(halo_shape)
        strips = got[:, halo_size:].reshape((nlon_dev,) + top.shape)
    else:
        west, east = exchange(
            [(pairs_from(-1, 0), stack[:, cells_lon - d :]), (pairs_from(1, 0), stack[:, :d])]
        )
        copies = jnp.broadcast_to(top[None], (nlon_dev,) + top.shape)
        strips = lax.all_to_all(copies, "lon", 0, 0) if small else None
    wide = jnp.concatenate([stack, east, west], axis=1)
    if lat_peers == 2:
        facing = jnp.where(is_top, wide[:, :, :d], wide[:, :, cells_lat - d :])
        sends = [([(k, k ^ 1) for k in range(2 * nlon_dev)], facing)]
    else:
        sends = [
            (pairs_from(0, -1), wide[:, :, cells_lat - d :]),
            (pairs_from(0, 1), wide[:, :, :d]),
        ]
    lat_got = exchange(sends)
    south, north = (lat_got[0], lat_got[0]) if lat_peers == 2 else lat_got

    if small:
        gathered = jnp.concatenate([strips[k] for k in range(nlon_dev)], axis=1)
    else:
        gathered = lax.all_gather(top, "lon", axis=1, tiled=True)
    base = 0
    pivot = fold_partner[0]
    first = (pivot - col0 - cells_lon - depth + 1 - base) % nlon
    doubled = jnp.concatenate([gathered[:, :nlon], gathered[:, :width]], axis=1)
    mirror = lax.dynamic_slice_in_dim(doubled, first, width, axis=1)[:, ::-1, ::-1]
    mirror = jnp.concatenate([mirror[:, d:], mirror[:, :d]], axis=1)
    north = jnp.where(is_top, mirror, north)

    lanes = -(-(cells_lat + 2 * d) // 128) * 128
    flags = jnp.stack([is_top, is_bottom]).astype(jnp.int32)
    vmem = pl.BlockSpec(memory_space=pltpu.VMEM)
    out = pl.pallas_call(
        lambda *refs: diffuse_kernel(*refs, nvar=nvar, nlev=nlev, depth=d),
        out_shape=jax.ShapeDtypeStruct((nfield, cells_lon, cells_lat), jnp.float32),
        in_specs=[pl.BlockSpec(memory_space=pltpu.SMEM)] + [vmem] * 6,
        out_specs=vmem,
        scratch_shapes=[pltpu.VMEM((stack.shape[0], width, lanes), jnp.float32)],
    )(flags, stack, east, west, north, south, error_std.reshape(nfield, cells_lon, cells_lat))
    return out.reshape(control.shape)


def diffuse_kernel(
    flags_ref, own_ref, east_ref, west_ref, north_ref, south_ref, std_ref, out_ref, ext_ref,
    *, nvar, nlev, depth
):
    nfield = nvar * nlev
    cells_lon, cells_lat = own_ref.shape[1:]
    width, lanes = ext_ref.shape[1], ext_ref.shape[2]
    is_top = flags_ref[0] == 1
    is_bottom = flags_ref[1] == 1
    ext_ref[:, :, cells_lat:] = jnp.zeros((ext_ref.shape[0], width, lanes - cells_lat), jnp.float32)
    ext_ref[:, :cells_lon, :cells_lat] = own_ref[...]
    ext_ref[:, cells_lon : cells_lon + depth, :cells_lat] = east_ref[...]
    ext_ref[:, cells_lon + depth :, :cells_lat] = west_ref[...]
    ext_ref[:, :, cells_lat : cells_lat + depth] = north_ref[...]
    ext_ref[:, :, lanes - depth :] = south_ref[...]

    def next_col(x):
        return pltpu.roll(x, width - 1, 0)

    def next_row(x):
        return pltpu.roll(x, lanes - 1, 1)

    row = lax.broadcasted_iota(jnp.int32, (width, lanes), 1)
    virtual = is_top & (row >= cells_lat) & (row < cells_lat + depth)
    fold_row = is_top & (row == cells_lat - 1)
    south_edge = is_bottom & (row == lanes - 1)
    kappa_e = ext_ref[nfield + nlev]
    kappa_n = ext_ref[nfield + nlev + 1]
    kappa_e = jnp.where(virtual, next_col(kappa_e), kappa_e)
    kappa_up = next_row(kappa_n)
    kappa_n = jnp.where(virtual, kappa_up, jnp.where(fold_row, 0.5 * (kappa_n + kappa_up), kappa_n))
    for lev in range(nlev):
        mask = ext_ref[nfield + lev]
        coef_e = kappa_e * mask * next_col(mask)
        coef_n = jnp.where(south_edge, 0.0, kappa_n * mask * next_row(mask))
        for var in range(nvar):
            plane = var * nlev + lev
            v = ext_ref[plane]
            for sweep in range(STEPS):
                flux_e = coef_e * (next_col(v) - v)
                flux_n = coef_n * (next_row(v) - v)
                v = v + (flux_e - pltpu.roll(flux_e, 1, 0)) + (flux_n - pltpu.roll(flux_n, 1, 1))
            out_ref[plane] = std_ref[plane] * v[:cells_lon, :cells_lat]


def solution(mesh):
    return jax.shard_map(
        per_device,
        mesh=mesh,
        in_specs=(
            P("ens", None, "lon", "lat"),
            P(None, None, "lon", "lat"),
            P(None, "lon", "lat"),
            P("lon", "lat"),
            P("lon", "lat"),
            P(),
        ),
        out_specs=P("ens", None, "lon", "lat"),
        check_vma=False,
    )
```

```python
import jax
import jax.numpy as jnp
from jax import lax
from jax.experimental import pallas as pl
from jax.experimental.pallas import tpu as pltpu
from jax.sharding import PartitionSpec as P

STEPS = 8


AXES = ("lon", "lat")


def exchange(sends):
    groups = {}
    for k, (pairs, x) in enumerate(sends):
        groups.setdefault(tuple(pairs), []).append(k)
    out = [None] * len(sends)
    for pairs, members in groups.items():
        if len(members) == 1:
            out[members[0]] = lax.ppermute(sends[members[0]][1], AXES, list(pairs))
            continue
        flat = jnp.concatenate([sends[k][1].reshape(-1) for k in members])
        got = lax.ppermute(flat, AXES, list(pairs))
        offset = 0
        for k in members:
            size = sends[k][1].size
            out[k] = got[offset : offset + size].reshape(sends[k][1].shape)
            offset += size
    return out


def pairs_from(d_lon, d_lat, lats=None):
    nlon, nlat = lax.axis_size("lon"), lax.axis_size("lat")
    pairs = []
    for lon in range(nlon):
        for lat in range(nlat) if lats is None else lats:
            dst = lat - d_lat
            if 0 <= dst < nlat:
                pairs.append((lon * nlat + lat, ((lon - d_lon) % nlon) * nlat + dst))
    return pairs


def per_device(control, error_std, land_mask, diff_east, diff_north, fold_partner):
    nvar, nlev, cells_lon, cells_lat = control.shape
    depth = STEPS
    nlon = fold_partner.shape[0]
    width = cells_lon + 2 * depth
    rows = cells_lat + 2 * depth
    nfield = nvar * nlev
    lat_index, lat_peers = lax.axis_index("lat"), lax.axis_size("lat")
    is_top = lat_index == lat_peers - 1
    is_bottom = lat_index == 0
    col0 = lax.axis_index("lon") * cells_lon

    field = (error_std * control).reshape(nfield, cells_lon, cells_lat)
    stack = jnp.concatenate(
        [field, land_mask.astype(jnp.float32), diff_east[None], diff_north[None]], axis=0
    )

    nlon_dev = lax.axis_size("lon")
    d = depth
    top = stack[:, :, cells_lat - d :]
    small = nlon_dev <= 16
    west, east = exchange(
        [(pairs_from(-1, 0), stack[:, cells_lon - d :]), (pairs_from(1, 0), stack[:, :d])]
    )
    wide = jnp.concatenate([stack, east, west], axis=1)
    if lat_peers == 2:
        facing = jnp.where(is_top, wide[:, :, :d], wide[:, :, cells_lat - d :])
        sends = [([(k, k ^ 1) for k in range(2 * nlon_dev)], facing)]
    else:
        sends = [
            (pairs_from(0, -1), wide[:, :, cells_lat - d :]),
            (pairs_from(0, 1), wide[:, :, :d]),
        ]
    lat_got = exchange(sends)
    south, north = (lat_got[0], lat_got[0]) if lat_peers == 2 else lat_got

    if small:
        copies = jnp.broadcast_to(top[None], (nlon_dev,) + top.shape)
        gathered = lax.all_to_all(copies, "lon", 0, 2, tiled=True)[0]
    else:
        gathered = lax.all_gather(top, "lon", axis=1, tiled=True)
    base = 0
    pivot = fold_partner[0]
    first = (pivot - col0 - cells_lon - depth + 1 - base) % nlon
    doubled = jnp.concatenate([gathered[:, :nlon], gathered[:, :width]], axis=1)
    mirror = lax.dynamic_slice_in_dim(doubled, first, width, axis=1)[:, ::-1, ::-1]
    mirror = jnp.concatenate([mirror[:, d:], mirror[:, :d]], axis=1)
    north = jnp.where(is_top, mirror, north)

    lanes = -(-(cells_lat + 2 * d) // 128) * 128
    flags = jnp.stack([is_top, is_bottom]).astype(jnp.int32)
    vmem = pl.BlockSpec(memory_space=pltpu.VMEM)
    out = pl.pallas_call(
        lambda *refs: diffuse_kernel(*refs, nvar=nvar, nlev=nlev, depth=d),
        out_shape=jax.ShapeDtypeStruct((nfield, cells_lon, cells_lat), jnp.float32),
        in_specs=[pl.BlockSpec(memory_space=pltpu.SMEM)] + [vmem] * 6,
        out_specs=vmem,
        scratch_shapes=[pltpu.VMEM((stack.shape[0], width, lanes), jnp.float32)],
    )(flags, stack, east, west, north, south, error_std.reshape(nfield, cells_lon, cells_lat))
    return out.reshape(control.shape)


def diffuse_kernel(
    flags_ref, own_ref, east_ref, west_ref, north_ref, south_ref, std_ref, out_ref, ext_ref,
    *, nvar, nlev, depth
):
    nfield = nvar * nlev
    cells_lon, cells_lat = own_ref.shape[1:]
    width, lanes = ext_ref.shape[1], ext_ref.shape[2]
    is_top = flags_ref[0] == 1
    is_bottom = flags_ref[1] == 1
    ext_ref[:, :, cells_lat:] = jnp.zeros((ext_ref.shape[0], width, lanes - cells_lat), jnp.float32)
    ext_ref[:, :cells_lon, :cells_lat] = own_ref[...]
    ext_ref[:, cells_lon : cells_lon + depth, :cells_lat] = east_ref[...]
    ext_ref[:, cells_lon + depth :, :cells_lat] = west_ref[...]
    ext_ref[:, :, cells_lat : cells_lat + depth] = north_ref[...]
    ext_ref[:, :, lanes - depth :] = south_ref[...]

    def next_col(x):
        return pltpu.roll(x, width - 1, 0)

    def next_row(x):
        return pltpu.roll(x, lanes - 1, 1)

    row = lax.broadcasted_iota(jnp.int32, (width, lanes), 1)
    virtual = is_top & (row >= cells_lat) & (row < cells_lat + depth)
    fold_row = is_top & (row == cells_lat - 1)
    south_edge = is_bottom & (row == lanes - 1)
    kappa_e = ext_ref[nfield + nlev]
    kappa_n = ext_ref[nfield + nlev + 1]
    kappa_e = jnp.where(virtual, next_col(kappa_e), kappa_e)
    kappa_up = next_row(kappa_n)
    kappa_n = jnp.where(virtual, kappa_up, jnp.where(fold_row, 0.5 * (kappa_n + kappa_up), kappa_n))
    for lev in range(nlev):
        mask = ext_ref[nfield + lev]
        coef_e = kappa_e * mask * next_col(mask)
        coef_n = jnp.where(south_edge, 0.0, kappa_n * mask * next_row(mask))
        for var in range(nvar):
            plane = var * nlev + lev
            v = ext_ref[plane]
            for sweep in range(STEPS):
                flux_e = coef_e * (next_col(v) - v)
                flux_n = coef_n * (next_row(v) - v)
                v = v + (flux_e - pltpu.roll(flux_e, 1, 0)) + (flux_n - pltpu.roll(flux_n, 1, 1))
            out_ref[plane] = std_ref[plane] * v[:cells_lon, :cells_lat]


def solution(mesh):
    return jax.shard_map(
        per_device,
        mesh=mesh,
        in_specs=(
            P("ens", None, "lon", "lat"),
            P(None, None, "lon", "lat"),
            P(None, "lon", "lat"),
            P("lon", "lat"),
            P("lon", "lat"),
            P(),
        ),
        out_specs=P("ens", None, "lon", "lat"),
        check_vma=False,
    )
```

```python
import jax
import jax.numpy as jnp
from jax import lax
from jax.experimental import pallas as pl
from jax.experimental.pallas import tpu as pltpu
from jax.sharding import PartitionSpec as P

STEPS = 8


AXES = ("lon", "lat")


def exchange(sends):
    groups = {}
    for k, (pairs, x) in enumerate(sends):
        groups.setdefault(tuple(pairs), []).append(k)
    out = [None] * len(sends)
    for pairs, members in groups.items():
        if len(members) == 1:
            out[members[0]] = lax.ppermute(sends[members[0]][1], AXES, list(pairs))
            continue
        flat = jnp.concatenate([sends[k][1].reshape(-1) for k in members])
        got = lax.ppermute(flat, AXES, list(pairs))
        offset = 0
        for k in members:
            size = sends[k][1].size
            out[k] = got[offset : offset + size].reshape(sends[k][1].shape)
            offset += size
    return out


def pairs_from(d_lon, d_lat, lats=None):
    nlon, nlat = lax.axis_size("lon"), lax.axis_size("lat")
    pairs = []
    for lon in range(nlon):
        for lat in range(nlat) if lats is None else lats:
            dst = lat - d_lat
            if 0 <= dst < nlat:
                pairs.append((lon * nlat + lat, ((lon - d_lon) % nlon) * nlat + dst))
    return pairs


def per_device(control, error_std, land_mask, diff_east, diff_north, fold_partner):
    nvar, nlev, cells_lon, cells_lat = control.shape
    depth = STEPS
    nlon = fold_partner.shape[0]
    width = cells_lon + 2 * depth
    rows = cells_lat + 2 * depth
    nfield = nvar * nlev
    lat_index, lat_peers = lax.axis_index("lat"), lax.axis_size("lat")
    is_top = lat_index == lat_peers - 1
    is_bottom = lat_index == 0
    col0 = lax.axis_index("lon") * cells_lon

    field = (error_std * control).reshape(nfield, cells_lon, cells_lat)
    stack = jnp.concatenate(
        [field, land_mask.astype(jnp.float32), diff_east[None], diff_north[None]], axis=0
    )

    nlon_dev = lax.axis_size("lon")
    d = depth
    top = stack[:, :, cells_lat - d :]
    small = nlon_dev <= 16
    west, east = exchange(
        [(pairs_from(-1, 0), stack[:, cells_lon - d :]), (pairs_from(1, 0), stack[:, :d])]
    )
    wide = jnp.concatenate([stack, east, west], axis=1)
    if lat_peers == 2:
        facing = jnp.where(is_top, wide[:, :, :d], wide[:, :, cells_lat - d :])
        sends = [([(k, k ^ 1) for k in range(2 * nlon_dev)], facing)]
    else:
        sends = [
            (pairs_from(0, -1), wide[:, :, cells_lat - d :]),
            (pairs_from(0, 1), wide[:, :, :d]),
        ]
    lat_got = exchange(sends)
    south, north = (lat_got[0], lat_got[0]) if lat_peers == 2 else lat_got

    if small:
        copies = jnp.broadcast_to(top[None], (nlon_dev,) + top.shape)
        gathered = lax.all_to_all(copies, "lon", 0, 2, tiled=True)[0]
    else:
        gathered = lax.all_gather(top, "lon", axis=1, tiled=True)
    base = 0
    pivot = fold_partner[0]
    first = (pivot - col0 - cells_lon - depth + 1 - base) % nlon
    doubled = jnp.concatenate([gathered[:, :nlon], gathered[:, :width]], axis=1)
    mirror = lax.dynamic_slice_in_dim(doubled, first, width, axis=1)[:, ::-1, ::-1]
    mirror = jnp.concatenate([mirror[:, d:], mirror[:, :d]], axis=1)
    lanes = -(-(cells_lat + 2 * d) // 128) * 128
    flags = jnp.stack([is_top, is_bottom]).astype(jnp.int32)
    smem = pl.BlockSpec(memory_space=pltpu.SMEM)
    vmem = pl.BlockSpec(memory_space=pltpu.VMEM)
    std = error_std.reshape(nfield, cells_lon, cells_lat)
    out = pl.pallas_call(
        lambda *refs: diffuse_kernel(*refs, nvar=nvar, nlev=nlev, depth=d),
        out_shape=jax.ShapeDtypeStruct((nfield, cells_lon, cells_lat), jnp.float32),
        in_specs=[smem] + [vmem] * 6,
        out_specs=vmem,
        scratch_shapes=[pltpu.VMEM((stack.shape[0], width, lanes), jnp.float32)],
    )(flags, stack, east, west, north, south, std)
    band = pl.pallas_call(
        lambda *refs: band_kernel(*refs, nvar=nvar, nlev=nlev, depth=d),
        out_shape=jax.ShapeDtypeStruct((nfield, cells_lon, d), jnp.float32),
        in_specs=[smem] + [vmem] * 5,
        out_specs=vmem,
        scratch_shapes=[pltpu.VMEM((stack.shape[0], width, 128), jnp.float32)],
    )(flags, stack, east, west, north, mirror)
    out = out.at[:, :, cells_lat - d :].set(std[:, :, cells_lat - d :] * band)
    return out.reshape(control.shape)


def sweep(ext_ref, flags_ref, own_rows, nvar, nlev, depth, south_open, emit):
    nfield = nvar * nlev
    width, lanes = ext_ref.shape[1], ext_ref.shape[2]
    is_top = flags_ref[0] == 1
    is_bottom = flags_ref[1] == 1

    def next_col(x):
        return pltpu.roll(x, width - 1, 0)

    def next_row(x):
        return pltpu.roll(x, lanes - 1, 1)

    row = lax.broadcasted_iota(jnp.int32, (width, lanes), 1)
    virtual = is_top & (row >= own_rows) & (row < own_rows + depth)
    fold_row = is_top & (row == own_rows - 1)
    south_edge = is_bottom & (row == lanes - 1) & south_open
    kappa_e = ext_ref[nfield + nlev]
    kappa_n = ext_ref[nfield + nlev + 1]
    kappa_e = jnp.where(virtual, next_col(kappa_e), kappa_e)
    kappa_up = next_row(kappa_n)
    kappa_n = jnp.where(virtual, kappa_up, jnp.where(fold_row, 0.5 * (kappa_n + kappa_up), kappa_n))
    for lev in range(nlev):
        mask = ext_ref[nfield + lev]
        coef_e = kappa_e * mask * next_col(mask)
        coef_n = jnp.where(south_edge, 0.0, kappa_n * mask * next_row(mask))
        for var in range(nvar):
            plane = var * nlev + lev
            v = ext_ref[plane]
            for step in range(STEPS):
                flux_e = coef_e * (next_col(v) - v)
                flux_n = coef_n * (next_row(v) - v)
                v = v + (flux_e - pltpu.roll(flux_e, 1, 0)) + (flux_n - pltpu.roll(flux_n, 1, 1))
            emit(plane, v)


def diffuse_kernel(
    flags_ref, own_ref, east_ref, west_ref, north_ref, south_ref, std_ref, out_ref, ext_ref,
    *, nvar, nlev, depth
):
    cells_lon, cells_lat = own_ref.shape[1:]
    width, lanes = ext_ref.shape[1], ext_ref.shape[2]
    ext_ref[:, :, cells_lat:] = jnp.zeros((ext_ref.shape[0], width, lanes - cells_lat), jnp.float32)
    ext_ref[:, :cells_lon, :cells_lat] = own_ref[...]
    ext_ref[:, cells_lon : cells_lon + depth, :cells_lat] = east_ref[...]
    ext_ref[:, cells_lon + depth :, :cells_lat] = west_ref[...]
    ext_ref[:, :, cells_lat : cells_lat + depth] = north_ref[...]
    ext_ref[:, :, lanes - depth :] = south_ref[...]

    def emit(plane, v):
        out_ref[plane] = std_ref[plane] * v[:cells_lon, :cells_lat]

    sweep(ext_ref, flags_ref, cells_lat, nvar, nlev, depth, True, emit)


def band_kernel(
    flags_ref, own_ref, east_ref, west_ref, north_ref, mirror_ref, out_ref, ext_ref,
    *, nvar, nlev, depth
):
    cells_lon, cells_lat = own_ref.shape[1:]
    rows = 2 * depth
    is_top = flags_ref[0] == 1
    ext_ref[:, :, rows:] = jnp.zeros((ext_ref.shape[0], ext_ref.shape[1], ext_ref.shape[2] - rows), jnp.float32)
    ext_ref[:, :cells_lon, :rows] = own_ref[:, :, cells_lat - rows :]
    ext_ref[:, cells_lon : cells_lon + depth, :rows] = east_ref[:, :, cells_lat - rows :]
    ext_ref[:, cells_lon + depth :, :rows] = west_ref[:, :, cells_lat - rows :]
    ext_ref[:, :, rows : rows + depth] = jnp.where(is_top, mirror_ref[...], north_ref[...])

    def emit(plane, v):
        out_ref[plane] = v[:cells_lon, depth:rows]

    sweep(ext_ref, flags_ref, rows, nvar, nlev, depth, False, emit)


def solution(mesh):
    return jax.shard_map(
        per_device,
        mesh=mesh,
        in_specs=(
            P("ens", None, "lon", "lat"),
            P(None, None, "lon", "lat"),
            P(None, "lon", "lat"),
            P("lon", "lat"),
            P("lon", "lat"),
            P(),
        ),
        out_specs=P("ens", None, "lon", "lat"),
        check_vma=False,
    )
```

```python
import jax
import jax.numpy as jnp
from jax import lax
from jax.experimental import pallas as pl
from jax.experimental.pallas import tpu as pltpu
from jax.sharding import PartitionSpec as P

STEPS = 8


AXES = ("lon", "lat")


def exchange(sends):
    groups = {}
    for k, (pairs, x) in enumerate(sends):
        groups.setdefault(tuple(pairs), []).append(k)
    out = [None] * len(sends)
    for pairs, members in groups.items():
        if len(members) == 1:
            out[members[0]] = lax.ppermute(sends[members[0]][1], AXES, list(pairs))
            continue
        flat = jnp.concatenate([sends[k][1].reshape(-1) for k in members])
        got = lax.ppermute(flat, AXES, list(pairs))
        offset = 0
        for k in members:
            size = sends[k][1].size
            out[k] = got[offset : offset + size].reshape(sends[k][1].shape)
            offset += size
    return out


def pairs_from(d_lon, d_lat, lats=None):
    nlon, nlat = lax.axis_size("lon"), lax.axis_size("lat")
    pairs = []
    for lon in range(nlon):
        for lat in range(nlat) if lats is None else lats:
            dst = lat - d_lat
            if 0 <= dst < nlat:
                pairs.append((lon * nlat + lat, ((lon - d_lon) % nlon) * nlat + dst))
    return pairs


def per_device(control, error_std, land_mask, diff_east, diff_north, fold_partner):
    nvar, nlev, cells_lon, cells_lat = control.shape
    depth = STEPS
    nlon = fold_partner.shape[0]
    width = cells_lon + 2 * depth
    rows = cells_lat + 2 * depth
    nfield = nvar * nlev
    lat_index, lat_peers = lax.axis_index("lat"), lax.axis_size("lat")
    is_top = lat_index == lat_peers - 1
    is_bottom = lat_index == 0
    col0 = lax.axis_index("lon") * cells_lon

    field = (error_std * control).reshape(nfield, cells_lon, cells_lat)
    stack = jnp.concatenate(
        [field, land_mask.astype(jnp.float32), diff_east[None], diff_north[None]], axis=0
    )

    nlon_dev = lax.axis_size("lon")
    d = depth
    top = stack[:, :, cells_lat - d :]
    small = nlon_dev <= 16
    west, east = exchange(
        [(pairs_from(-1, 0), stack[:, cells_lon - d :]), (pairs_from(1, 0), stack[:, :d])]
    )
    wide = jnp.concatenate([stack, east, west], axis=1)
    if lat_peers == 2:
        facing = jnp.where(is_top, wide[:, :, :d], wide[:, :, cells_lat - d :])
        sends = [([(k, k ^ 1) for k in range(2 * nlon_dev)], facing)]
    else:
        sends = [
            (pairs_from(0, -1), wide[:, :, cells_lat - d :]),
            (pairs_from(0, 1), wide[:, :, :d]),
        ]
    lat_got = exchange(sends)
    south, north = (lat_got[0], lat_got[0]) if lat_peers == 2 else lat_got

    if small:
        copies = jnp.broadcast_to(top[None], (nlon_dev,) + top.shape)
        gathered = lax.all_to_all(copies, "lon", 0, 2, tiled=True)[0]
    else:
        gathered = lax.all_gather(top, "lon", axis=1, tiled=True)
    base = 0
    pivot = fold_partner[0]
    first = (pivot - col0 - cells_lon - depth + 1 - base) % nlon
    doubled = jnp.concatenate([gathered[:, :nlon], gathered[:, :width]], axis=1)
    mirror = lax.dynamic_slice_in_dim(doubled, first, width, axis=1)[:, ::-1, ::-1]
    mirror = jnp.concatenate([mirror[:, d:], mirror[:, :d]], axis=1)
    north = jnp.where(is_top, mirror, north)

    lanes = -(-(cells_lat + 2 * d) // 128) * 128
    flags = jnp.stack([is_top, is_bottom]).astype(jnp.int32)
    vmem = pl.BlockSpec(memory_space=pltpu.VMEM)
    out = pl.pallas_call(
        lambda *refs: diffuse_kernel(*refs, nvar=nvar, nlev=nlev, depth=d),
        out_shape=jax.ShapeDtypeStruct((nfield, cells_lon, cells_lat), jnp.float32),
        in_specs=[pl.BlockSpec(memory_space=pltpu.SMEM)] + [vmem] * 6,
        out_specs=vmem,
        scratch_shapes=[pltpu.VMEM((stack.shape[0], width, lanes), jnp.float32)],
    )(flags, stack, east, west, north, south, error_std.reshape(nfield, cells_lon, cells_lat))
    return out.reshape(control.shape)


def diffuse_kernel(
    flags_ref, own_ref, east_ref, west_ref, north_ref, south_ref, std_ref, out_ref, ext_ref,
    *, nvar, nlev, depth
):
    nfield = nvar * nlev
    cells_lon, cells_lat = own_ref.shape[1:]
    width, lanes = ext_ref.shape[1], ext_ref.shape[2]
    is_top = flags_ref[0] == 1
    is_bottom = flags_ref[1] == 1
    ext_ref[:, :, cells_lat:] = jnp.zeros((ext_ref.shape[0], width, lanes - cells_lat), jnp.float32)
    ext_ref[:, :cells_lon, :cells_lat] = own_ref[...]
    ext_ref[:, cells_lon : cells_lon + depth, :cells_lat] = east_ref[...]
    ext_ref[:, cells_lon + depth :, :cells_lat] = west_ref[...]
    ext_ref[:, :, cells_lat : cells_lat + depth] = north_ref[...]
    ext_ref[:, :, lanes - depth :] = south_ref[...]

    def next_col(x):
        return pltpu.roll(x, width - 1, 0)

    def next_row(x):
        return pltpu.roll(x, lanes - 1, 1)

    row = lax.broadcasted_iota(jnp.int32, (width, lanes), 1)
    virtual = is_top & (row >= cells_lat) & (row < cells_lat + depth)
    fold_row = is_top & (row == cells_lat - 1)
    south_edge = is_bottom & (row == lanes - 1)
    kappa_e = ext_ref[nfield + nlev]
    kappa_n = ext_ref[nfield + nlev + 1]
    kappa_e = jnp.where(virtual, next_col(kappa_e), kappa_e)
    kappa_up = next_row(kappa_n)
    kappa_n = jnp.where(virtual, kappa_up, jnp.where(fold_row, 0.5 * (kappa_n + kappa_up), kappa_n))
    coef_e, coef_n = [], []
    for lev in range(nlev):
        mask = ext_ref[nfield + lev]
        coef_e.append(kappa_e * mask * next_col(mask))
        coef_n.append(jnp.where(south_edge, 0.0, kappa_n * mask * next_row(mask)))
    fields = [ext_ref[plane] for plane in range(nfield)]
    for sweep in range(STEPS):
        for plane in range(nfield):
            v, lev = fields[plane], plane % nlev
            flux_e = coef_e[lev] * (next_col(v) - v)
            flux_n = coef_n[lev] * (next_row(v) - v)
            fields[plane] = v + (flux_e - pltpu.roll(flux_e, 1, 0)) + (flux_n - pltpu.roll(flux_n, 1, 1))
    for plane in range(nfield):
        out_ref[plane] = std_ref[plane] * fields[plane][:cells_lon, :cells_lat]


def solution(mesh):
    return jax.shard_map(
        per_device,
        mesh=mesh,
        in_specs=(
            P("ens", None, "lon", "lat"),
            P(None, None, "lon", "lat"),
            P(None, "lon", "lat"),
            P("lon", "lat"),
            P("lon", "lat"),
            P(),
        ),
        out_specs=P("ens", None, "lon", "lat"),
        check_vma=False,
    )
```

```python
import jax
import jax.numpy as jnp
from jax import lax
from jax.experimental import pallas as pl
from jax.experimental.pallas import tpu as pltpu
from jax.sharding import PartitionSpec as P

STEPS = 8


AXES = ("lon", "lat")


def exchange(sends):
    groups = {}
    for k, (pairs, x) in enumerate(sends):
        groups.setdefault(tuple(pairs), []).append(k)
    out = [None] * len(sends)
    for pairs, members in groups.items():
        if len(members) == 1:
            out[members[0]] = lax.ppermute(sends[members[0]][1], AXES, list(pairs))
            continue
        flat = jnp.concatenate([sends[k][1].reshape(-1) for k in members])
        got = lax.ppermute(flat, AXES, list(pairs))
        offset = 0
        for k in members:
            size = sends[k][1].size
            out[k] = got[offset : offset + size].reshape(sends[k][1].shape)
            offset += size
    return out


def pairs_from(d_lon, d_lat, lats=None):
    nlon, nlat = lax.axis_size("lon"), lax.axis_size("lat")
    pairs = []
    for lon in range(nlon):
        for lat in range(nlat) if lats is None else lats:
            dst = lat - d_lat
            if 0 <= dst < nlat:
                pairs.append((lon * nlat + lat, ((lon - d_lon) % nlon) * nlat + dst))
    return pairs


def per_device(control, error_std, land_mask, diff_east, diff_north, fold_partner):
    nvar, nlev, cells_lon, cells_lat = control.shape
    depth = STEPS
    nlon = fold_partner.shape[0]
    width = cells_lon + 2 * depth
    rows = cells_lat + 2 * depth
    nfield = nvar * nlev
    lat_index, lat_peers = lax.axis_index("lat"), lax.axis_size("lat")
    is_top = lat_index == lat_peers - 1
    is_bottom = lat_index == 0
    col0 = lax.axis_index("lon") * cells_lon

    field = (error_std * control).reshape(nfield, cells_lon, cells_lat)
    stack = jnp.concatenate(
        [field, land_mask.astype(jnp.float32), diff_east[None], diff_north[None]], axis=0
    )

    nlon_dev = lax.axis_size("lon")
    d = depth
    tail = slice(cells_lat - d, None)
    top = jnp.concatenate(
        [
            (error_std[..., tail] * control[..., tail]).reshape(nfield, cells_lon, d),
            land_mask[..., tail].astype(jnp.float32),
            diff_east[None, :, tail],
            diff_north[None, :, tail],
        ],
        axis=0,
    )
    small = nlon_dev <= 16
    west, east = exchange(
        [(pairs_from(-1, 0), stack[:, cells_lon - d :]), (pairs_from(1, 0), stack[:, :d])]
    )
    wide = jnp.concatenate([stack, east, west], axis=1)
    if lat_peers == 2:
        facing = jnp.where(is_top, wide[:, :, :d], wide[:, :, cells_lat - d :])
        sends = [([(k, k ^ 1) for k in range(2 * nlon_dev)], facing)]
    else:
        sends = [
            (pairs_from(0, -1), wide[:, :, cells_lat - d :]),
            (pairs_from(0, 1), wide[:, :, :d]),
        ]
    lat_got = exchange(sends)
    south, north = (lat_got[0], lat_got[0]) if lat_peers == 2 else lat_got

    if small:
        copies = jnp.broadcast_to(top[None], (nlon_dev,) + top.shape)
        gathered = lax.all_to_all(copies, "lon", 0, 2, tiled=True)[0]
    else:
        gathered = lax.all_gather(top, "lon", axis=1, tiled=True)
    base = 0
    pivot = fold_partner[0]
    first = (pivot - col0 - cells_lon - depth + 1 - base) % nlon
    doubled = jnp.concatenate([gathered[:, :nlon], gathered[:, :width]], axis=1)
    mirror = lax.dynamic_slice_in_dim(doubled, first, width, axis=1)[:, ::-1, ::-1]
    mirror = jnp.concatenate([mirror[:, d:], mirror[:, :d]], axis=1)
    north = jnp.where(is_top, mirror, north)

    lanes = -(-(cells_lat + 2 * d) // 128) * 128
    flags = jnp.stack([is_top, is_bottom]).astype(jnp.int32)
    vmem = pl.BlockSpec(memory_space=pltpu.VMEM)
    out = pl.pallas_call(
        lambda *refs: diffuse_kernel(*refs, nvar=nvar, nlev=nlev, depth=d),
        out_shape=jax.ShapeDtypeStruct((nfield, cells_lon, cells_lat), jnp.float32),
        in_specs=[pl.BlockSpec(memory_space=pltpu.SMEM)] + [vmem] * 6,
        out_specs=vmem,
        scratch_shapes=[pltpu.VMEM((stack.shape[0], width, lanes), jnp.float32)],
    )(flags, stack, east, west, north, south, error_std.reshape(nfield, cells_lon, cells_lat))
    return out.reshape(control.shape)


def diffuse_kernel(
    flags_ref, own_ref, east_ref, west_ref, north_ref, south_ref, std_ref, out_ref, ext_ref,
    *, nvar, nlev, depth
):
    nfield = nvar * nlev
    cells_lon, cells_lat = own_ref.shape[1:]
    width, lanes = ext_ref.shape[1], ext_ref.shape[2]
    is_top = flags_ref[0] == 1
    is_bottom = flags_ref[1] == 1
    ext_ref[:, :, cells_lat:] = jnp.zeros((ext_ref.shape[0], width, lanes - cells_lat), jnp.float32)
    ext_ref[:, :cells_lon, :cells_lat] = own_ref[...]
    ext_ref[:, cells_lon : cells_lon + depth, :cells_lat] = east_ref[...]
    ext_ref[:, cells_lon + depth :, :cells_lat] = west_ref[...]
    ext_ref[:, :, cells_lat : cells_lat + depth] = north_ref[...]
    ext_ref[:, :, lanes - depth :] = south_ref[...]

    def next_col(x):
        return pltpu.roll(x, width - 1, 0)

    def next_row(x):
        return pltpu.roll(x, lanes - 1, 1)

    row = lax.broadcasted_iota(jnp.int32, (width, lanes), 1)
    virtual = is_top & (row >= cells_lat) & (row < cells_lat + depth)
    fold_row = is_top & (row == cells_lat - 1)
    south_edge = is_bottom & (row == lanes - 1)
    kappa_e = ext_ref[nfield + nlev]
    kappa_n = ext_ref[nfield + nlev + 1]
    kappa_e = jnp.where(virtual, next_col(kappa_e), kappa_e)
    kappa_up = next_row(kappa_n)
    kappa_n = jnp.where(virtual, kappa_up, jnp.where(fold_row, 0.5 * (kappa_n + kappa_up), kappa_n))
    for lev in range(nlev):
        mask = ext_ref[nfield + lev]
        coef_e = kappa_e * mask * next_col(mask)
        coef_n = jnp.where(south_edge, 0.0, kappa_n * mask * next_row(mask))
        for var in range(nvar):
            plane = var * nlev + lev
            v = ext_ref[plane]
            for sweep in range(STEPS):
                flux_e = coef_e * (next_col(v) - v)
                flux_n = coef_n * (next_row(v) - v)
                v = v + (flux_e - pltpu.roll(flux_e, 1, 0)) + (flux_n - pltpu.roll(flux_n, 1, 1))
            out_ref[plane] = std_ref[plane] * v[:cells_lon, :cells_lat]


def solution(mesh):
    return jax.shard_map(
        per_device,
        mesh=mesh,
        in_specs=(
            P("ens", None, "lon", "lat"),
            P(None, None, "lon", "lat"),
            P(None, "lon", "lat"),
            P("lon", "lat"),
            P("lon", "lat"),
            P(),
        ),
        out_specs=P("ens", None, "lon", "lat"),
        check_vma=False,
    )
```

```python
import jax
import jax.numpy as jnp
from jax import lax
from jax.experimental import pallas as pl
from jax.experimental.pallas import tpu as pltpu
from jax.sharding import PartitionSpec as P

STEPS = 8


AXES = ("lon", "lat")


def exchange(sends):
    groups = {}
    for k, (pairs, x) in enumerate(sends):
        groups.setdefault(tuple(pairs), []).append(k)
    out = [None] * len(sends)
    for pairs, members in groups.items():
        if len(members) == 1:
            out[members[0]] = lax.ppermute(sends[members[0]][1], AXES, list(pairs))
            continue
        flat = jnp.concatenate([sends[k][1].reshape(-1) for k in members])
        got = lax.ppermute(flat, AXES, list(pairs))
        offset = 0
        for k in members:
            size = sends[k][1].size
            out[k] = got[offset : offset + size].reshape(sends[k][1].shape)
            offset += size
    return out


def pairs_from(d_lon, d_lat, lats=None):
    nlon, nlat = lax.axis_size("lon"), lax.axis_size("lat")
    pairs = []
    for lon in range(nlon):
        for lat in range(nlat) if lats is None else lats:
            dst = lat - d_lat
            if 0 <= dst < nlat:
                pairs.append((lon * nlat + lat, ((lon - d_lon) % nlon) * nlat + dst))
    return pairs


def per_device(control, error_std, land_mask, diff_east, diff_north, fold_partner):
    nvar, nlev, cells_lon, cells_lat = control.shape
    depth = STEPS
    nlon = fold_partner.shape[0]
    width = cells_lon + 2 * depth
    rows = cells_lat + 2 * depth
    nfield = nvar * nlev
    lat_index, lat_peers = lax.axis_index("lat"), lax.axis_size("lat")
    is_top = lat_index == lat_peers - 1
    is_bottom = lat_index == 0
    col0 = lax.axis_index("lon") * cells_lon

    field = (error_std * control).reshape(nfield, cells_lon, cells_lat)
    stack = jnp.concatenate(
        [field, land_mask.astype(jnp.float32), diff_east[None], diff_north[None]], axis=0
    )

    nlon_dev = lax.axis_size("lon")
    d = depth
    top = stack[:, :, cells_lat - d :]
    small = nlon_dev <= 16
    west, east = exchange(
        [(pairs_from(-1, 0), stack[:, cells_lon - d :]), (pairs_from(1, 0), stack[:, :d])]
    )
    wide = jnp.concatenate([stack, east, west], axis=1)
    if lat_peers == 2:
        facing = jnp.where(is_top, wide[:, :, :d], wide[:, :, cells_lat - d :])
        sends = [([(k, k ^ 1) for k in range(2 * nlon_dev)], facing)]
    else:
        sends = [
            (pairs_from(0, -1), wide[:, :, cells_lat - d :]),
            (pairs_from(0, 1), wide[:, :, :d]),
        ]
    lat_got = exchange(sends)
    south, north = (lat_got[0], lat_got[0]) if lat_peers == 2 else lat_got

    if small:
        copies = jnp.broadcast_to(top[None], (nlon_dev,) + top.shape)
        gathered = lax.all_to_all(copies, "lon", 0, 2, tiled=True)[0]
    else:
        gathered = lax.all_gather(top, "lon", axis=1, tiled=True)
    base = 0
    pivot = fold_partner[0]
    first = (pivot - col0 - cells_lon - depth + 1 - base) % nlon
    doubled = jnp.concatenate([gathered[:, :nlon], gathered[:, :width]], axis=1)
    mirror = lax.dynamic_slice_in_dim(doubled, first, width, axis=1)[:, ::-1, ::-1]
    mirror = jnp.concatenate([mirror[:, d:], mirror[:, :d]], axis=1)
    north = jnp.where(is_top, mirror, north)

    lanes = -(-(cells_lat + 2 * d) // 128) * 128
    flags = jnp.stack([is_top, is_bottom]).astype(jnp.int32)
    vmem = pl.BlockSpec(memory_space=pltpu.VMEM)
    out = pl.pallas_call(
        lambda *refs: diffuse_kernel(*refs, nvar=nvar, nlev=nlev, depth=d),
        out_shape=jax.ShapeDtypeStruct((nfield, cells_lon, cells_lat), jnp.float32),
        in_specs=[pl.BlockSpec(memory_space=pltpu.SMEM)] + [vmem] * 6,
        out_specs=vmem,
        scratch_shapes=[pltpu.VMEM((stack.shape[0], width, lanes), jnp.float32)],
    )(flags, stack, east, west, north, south, error_std.reshape(nfield, cells_lon, cells_lat))
    return out.reshape(control.shape)


def diffuse_kernel(
    flags_ref, own_ref, east_ref, west_ref, north_ref, south_ref, std_ref, out_ref, ext_ref,
    *, nvar, nlev, depth
):
    nfield = nvar * nlev
    cells_lon, cells_lat = own_ref.shape[1:]
    width, lanes = ext_ref.shape[1], ext_ref.shape[2]
    is_top = flags_ref[0] == 1
    is_bottom = flags_ref[1] == 1
    ext_ref[:, :, cells_lat:] = jnp.zeros((ext_ref.shape[0], width, lanes - cells_lat), jnp.float32)
    ext_ref[:, :cells_lon, :cells_lat] = own_ref[...]
    ext_ref[:, cells_lon : cells_lon + depth, :cells_lat] = east_ref[...]
    ext_ref[:, cells_lon + depth :, :cells_lat] = west_ref[...]
    ext_ref[:, :, cells_lat : cells_lat + depth] = north_ref[...]
    ext_ref[:, :, lanes - depth :] = south_ref[...]

    def next_col(x):
        return pltpu.roll(x, width - 1, 0)

    def next_row(x):
        return pltpu.roll(x, lanes - 1, 1)

    row = lax.broadcasted_iota(jnp.int32, (width, lanes), 1)
    virtual = is_top & (row >= cells_lat) & (row < cells_lat + depth)
    fold_row = is_top & (row == cells_lat - 1)
    south_edge = is_bottom & (row == lanes - 1)
    kappa_e = ext_ref[nfield + nlev]
    kappa_n = ext_ref[nfield + nlev + 1]
    kappa_e = jnp.where(virtual, next_col(kappa_e), kappa_e)
    kappa_up = next_row(kappa_n)
    kappa_n = jnp.where(virtual, kappa_up, jnp.where(fold_row, 0.5 * (kappa_n + kappa_up), kappa_n))
    for lev in range(nlev):
        mask = ext_ref[nfield + lev]
        coef_e = kappa_e * mask * next_col(mask)
        coef_n = jnp.where(south_edge, 0.0, kappa_n * mask * next_row(mask))
        for var in range(nvar):
            plane = var * nlev + lev

            def step(sweep, v, coef_e=coef_e, coef_n=coef_n):
                flux_e = coef_e * (next_col(v) - v)
                flux_n = coef_n * (next_row(v) - v)
                return v + (flux_e - pltpu.roll(flux_e, 1, 0)) + (flux_n - pltpu.roll(flux_n, 1, 1))

            v = lax.fori_loop(0, STEPS, step, ext_ref[plane])
            out_ref[plane] = std_ref[plane] * v[:cells_lon, :cells_lat]


def solution(mesh):
    return jax.shard_map(
        per_device,
        mesh=mesh,
        in_specs=(
            P("ens", None, "lon", "lat"),
            P(None, None, "lon", "lat"),
            P(None, "lon", "lat"),
            P("lon", "lat"),
            P("lon", "lat"),
            P(),
        ),
        out_specs=P("ens", None, "lon", "lat"),
        check_vma=False,
    )
```

```python
import jax
import jax.numpy as jnp
from jax import lax
from jax.experimental import pallas as pl
from jax.experimental.pallas import tpu as pltpu
from jax.sharding import PartitionSpec as P

STEPS = 8


AXES = ("lon", "lat")


def exchange(sends):
    groups = {}
    for k, (pairs, x) in enumerate(sends):
        groups.setdefault(tuple(pairs), []).append(k)
    out = [None] * len(sends)
    for pairs, members in groups.items():
        if len(members) == 1:
            out[members[0]] = lax.ppermute(sends[members[0]][1], AXES, list(pairs))
            continue
        flat = jnp.concatenate([sends[k][1].reshape(-1) for k in members])
        got = lax.ppermute(flat, AXES, list(pairs))
        offset = 0
        for k in members:
            size = sends[k][1].size
            out[k] = got[offset : offset + size].reshape(sends[k][1].shape)
            offset += size
    return out


def pairs_from(d_lon, d_lat, lats=None):
    nlon, nlat = lax.axis_size("lon"), lax.axis_size("lat")
    pairs = []
    for lon in range(nlon):
        for lat in range(nlat) if lats is None else lats:
            dst = lat - d_lat
            if 0 <= dst < nlat:
                pairs.append((lon * nlat + lat, ((lon - d_lon) % nlon) * nlat + dst))
    return pairs


def per_device(control, error_std, land_mask, diff_east, diff_north, fold_partner):
    nvar, nlev, cells_lon, cells_lat = control.shape
    depth = STEPS
    nlon = fold_partner.shape[0]
    width = cells_lon + 2 * depth
    rows = cells_lat + 2 * depth
    nfield = nvar * nlev
    lat_index, lat_peers = lax.axis_index("lat"), lax.axis_size("lat")
    is_top = lat_index == lat_peers - 1
    is_bottom = lat_index == 0
    col0 = lax.axis_index("lon") * cells_lon

    field = (error_std * control).reshape(nfield, cells_lon, cells_lat)
    stack = jnp.concatenate(
        [field, land_mask.astype(jnp.float32), diff_east[None], diff_north[None]], axis=0
    )

    nlon_dev = lax.axis_size("lon")
    d = depth
    top = stack[:, :, cells_lat - d :]
    small = nlon_dev <= 16
    west, east = exchange(
        [(pairs_from(-1, 0), stack[:, cells_lon - d :]), (pairs_from(1, 0), stack[:, :d])]
    )
    wide = jnp.concatenate([stack, east, west], axis=1)
    if lat_peers == 2:
        facing = jnp.where(is_top, wide[:, :, :d], wide[:, :, cells_lat - d :])
        sends = [([(k, k ^ 1) for k in range(2 * nlon_dev)], facing)]
    else:
        sends = [
            (pairs_from(0, -1), wide[:, :, cells_lat - d :]),
            (pairs_from(0, 1), wide[:, :, :d]),
        ]
    lat_got = exchange(sends)
    south, north = (lat_got[0], lat_got[0]) if lat_peers == 2 else lat_got

    if small:
        flat = top.reshape(top.shape[0], -1)
        copies = jnp.broadcast_to(flat[None], (nlon_dev,) + flat.shape)
        strips = lax.all_to_all(copies, "lon", 0, 0).reshape((nlon_dev,) + top.shape)
        gathered = jnp.transpose(strips, (1, 0, 2, 3)).reshape(
            top.shape[0], nlon_dev * cells_lon, d
        )
    else:
        gathered = lax.all_gather(top, "lon", axis=1, tiled=True)
    base = 0
    pivot = fold_partner[0]
    first = (pivot - col0 - cells_lon - depth + 1 - base) % nlon
    doubled = jnp.concatenate([gathered[:, :nlon], gathered[:, :width]], axis=1)
    mirror = lax.dynamic_slice_in_dim(doubled, first, width, axis=1)[:, ::-1, ::-1]
    mirror = jnp.concatenate([mirror[:, d:], mirror[:, :d]], axis=1)
    north = jnp.where(is_top, mirror, north)

    lanes = -(-(cells_lat + 2 * d) // 128) * 128
    flags = jnp.stack([is_top, is_bottom]).astype(jnp.int32)
    vmem = pl.BlockSpec(memory_space=pltpu.VMEM)
    out = pl.pallas_call(
        lambda *refs: diffuse_kernel(*refs, nvar=nvar, nlev=nlev, depth=d),
        out_shape=jax.ShapeDtypeStruct((nfield, cells_lon, cells_lat), jnp.float32),
        in_specs=[pl.BlockSpec(memory_space=pltpu.SMEM)] + [vmem] * 6,
        out_specs=vmem,
        scratch_shapes=[pltpu.VMEM((stack.shape[0], width, lanes), jnp.float32)],
    )(flags, stack, east, west, north, south, error_std.reshape(nfield, cells_lon, cells_lat))
    return out.reshape(control.shape)


def diffuse_kernel(
    flags_ref, own_ref, east_ref, west_ref, north_ref, south_ref, std_ref, out_ref, ext_ref,
    *, nvar, nlev, depth
):
    nfield = nvar * nlev
    cells_lon, cells_lat = own_ref.shape[1:]
    width, lanes = ext_ref.shape[1], ext_ref.shape[2]
    is_top = flags_ref[0] == 1
    is_bottom = flags_ref[1] == 1
    ext_ref[:, :, cells_lat:] = jnp.zeros((ext_ref.shape[0], width, lanes - cells_lat), jnp.float32)
    ext_ref[:, :cells_lon, :cells_lat] = own_ref[...]
    ext_ref[:, cells_lon : cells_lon + depth, :cells_lat] = east_ref[...]
    ext_ref[:, cells_lon + depth :, :cells_lat] = west_ref[...]
    ext_ref[:, :, cells_lat : cells_lat + depth] = north_ref[...]
    ext_ref[:, :, lanes - depth :] = south_ref[...]

    def next_col(x):
        return pltpu.roll(x, width - 1, 0)

    def next_row(x):
        return pltpu.roll(x, lanes - 1, 1)

    row = lax.broadcasted_iota(jnp.int32, (width, lanes), 1)
    virtual = is_top & (row >= cells_lat) & (row < cells_lat + depth)
    fold_row = is_top & (row == cells_lat - 1)
    south_edge = is_bottom & (row == lanes - 1)
    kappa_e = ext_ref[nfield + nlev]
    kappa_n = ext_ref[nfield + nlev + 1]
    kappa_e = jnp.where(virtual, next_col(kappa_e), kappa_e)
    kappa_up = next_row(kappa_n)
    kappa_n = jnp.where(virtual, kappa_up, jnp.where(fold_row, 0.5 * (kappa_n + kappa_up), kappa_n))
    for lev in range(nlev):
        mask = ext_ref[nfield + lev]
        coef_e = kappa_e * mask * next_col(mask)
        coef_n = jnp.where(south_edge, 0.0, kappa_n * mask * next_row(mask))
        for var in range(nvar):
            plane = var * nlev + lev
            v = ext_ref[plane]
            for sweep in range(STEPS):
                flux_e = coef_e * (next_col(v) - v)
                flux_n = coef_n * (next_row(v) - v)
                v = v + (flux_e - pltpu.roll(flux_e, 1, 0)) + (flux_n - pltpu.roll(flux_n, 1, 1))
            out_ref[plane] = std_ref[plane] * v[:cells_lon, :cells_lat]


def solution(mesh):
    return jax.shard_map(
        per_device,
        mesh=mesh,
        in_specs=(
            P("ens", None, "lon", "lat"),
            P(None, None, "lon", "lat"),
            P(None, "lon", "lat"),
            P("lon", "lat"),
            P("lon", "lat"),
            P(),
        ),
        out_specs=P("ens", None, "lon", "lat"),
        check_vma=False,
    )
```

```python
import jax
import jax.numpy as jnp
from jax import lax
from jax.experimental import pallas as pl
from jax.experimental.pallas import tpu as pltpu
from jax.sharding import PartitionSpec as P

STEPS = 8


AXES = ("lon", "lat")


def exchange(sends):
    groups = {}
    for k, (pairs, x) in enumerate(sends):
        groups.setdefault(tuple(pairs), []).append(k)
    out = [None] * len(sends)
    for pairs, members in groups.items():
        if len(members) == 1:
            out[members[0]] = lax.ppermute(sends[members[0]][1], AXES, list(pairs))
            continue
        flat = jnp.concatenate([sends[k][1].reshape(-1) for k in members])
        got = lax.ppermute(flat, AXES, list(pairs))
        offset = 0
        for k in members:
            size = sends[k][1].size
            out[k] = got[offset : offset + size].reshape(sends[k][1].shape)
            offset += size
    return out


def pairs_from(d_lon, d_lat, lats=None):
    nlon, nlat = lax.axis_size("lon"), lax.axis_size("lat")
    pairs = []
    for lon in range(nlon):
        for lat in range(nlat) if lats is None else lats:
            dst = lat - d_lat
            if 0 <= dst < nlat:
                pairs.append((lon * nlat + lat, ((lon - d_lon) % nlon) * nlat + dst))
    return pairs


def per_device(control, error_std, land_mask, diff_east, diff_north, fold_partner):
    nvar, nlev, cells_lon, cells_lat = control.shape
    depth = STEPS
    nlon = fold_partner.shape[0]
    width = cells_lon + 2 * depth
    rows = cells_lat + 2 * depth
    nfield = nvar * nlev
    lat_index, lat_peers = lax.axis_index("lat"), lax.axis_size("lat")
    is_top = lat_index == lat_peers - 1
    is_bottom = lat_index == 0
    col0 = lax.axis_index("lon") * cells_lon

    field = (error_std * control).reshape(nfield, cells_lon, cells_lat)
    stack = jnp.concatenate(
        [field, land_mask.astype(jnp.float32), diff_east[None], diff_north[None]], axis=0
    )

    nlon_dev = lax.axis_size("lon")
    d = depth
    top = stack[:, :, cells_lat - d :]
    small = nlon_dev <= 16
    west, east = exchange(
        [(pairs_from(-1, 0), stack[:, cells_lon - d :]), (pairs_from(1, 0), stack[:, :d])]
    )
    wide = jnp.concatenate([stack, east, west], axis=1)
    if lat_peers == 2:
        facing = jnp.where(is_top, wide[:, :, :d], wide[:, :, cells_lat - d :])
        sends = [([(k, k ^ 1) for k in range(2 * nlon_dev)], facing)]
    else:
        sends = [
            (pairs_from(0, -1), wide[:, :, cells_lat - d :]),
            (pairs_from(0, 1), wide[:, :, :d]),
        ]
    lat_got = exchange(sends)
    south, north = (lat_got[0], lat_got[0]) if lat_peers == 2 else lat_got

    if small:
        top, west, east = lax.optimization_barrier((top, west, east))
        flat = top.reshape(top.shape[0], -1)
        copies = jnp.broadcast_to(flat[None], (nlon_dev,) + flat.shape)
        strips = lax.all_to_all(copies, "lon", 0, 0).reshape((nlon_dev,) + top.shape)
        gathered = jnp.transpose(strips, (1, 0, 2, 3)).reshape(
            top.shape[0], nlon_dev * cells_lon, d
        )
    else:
        gathered = lax.all_gather(top, "lon", axis=1, tiled=True)
    base = 0
    pivot = fold_partner[0]
    first = (pivot - col0 - cells_lon - depth + 1 - base) % nlon
    doubled = jnp.concatenate([gathered[:, :nlon], gathered[:, :width]], axis=1)
    mirror = lax.dynamic_slice_in_dim(doubled, first, width, axis=1)[:, ::-1, ::-1]
    mirror = jnp.concatenate([mirror[:, d:], mirror[:, :d]], axis=1)
    north = jnp.where(is_top, mirror, north)

    lanes = -(-(cells_lat + 2 * d) // 128) * 128
    flags = jnp.stack([is_top, is_bottom]).astype(jnp.int32)
    vmem = pl.BlockSpec(memory_space=pltpu.VMEM)
    out = pl.pallas_call(
        lambda *refs: diffuse_kernel(*refs, nvar=nvar, nlev=nlev, depth=d),
        out_shape=jax.ShapeDtypeStruct((nfield, cells_lon, cells_lat), jnp.float32),
        in_specs=[pl.BlockSpec(memory_space=pltpu.SMEM)] + [vmem] * 6,
        out_specs=vmem,
        scratch_shapes=[pltpu.VMEM((stack.shape[0], width, lanes), jnp.float32)],
    )(flags, stack, east, west, north, south, error_std.reshape(nfield, cells_lon, cells_lat))
    return out.reshape(control.shape)


def diffuse_kernel(
    flags_ref, own_ref, east_ref, west_ref, north_ref, south_ref, std_ref, out_ref, ext_ref,
    *, nvar, nlev, depth
):
    nfield = nvar * nlev
    cells_lon, cells_lat = own_ref.shape[1:]
    width, lanes = ext_ref.shape[1], ext_ref.shape[2]
    is_top = flags_ref[0] == 1
    is_bottom = flags_ref[1] == 1
    ext_ref[:, :, cells_lat:] = jnp.zeros((ext_ref.shape[0], width, lanes - cells_lat), jnp.float32)
    ext_ref[:, :cells_lon, :cells_lat] = own_ref[...]
    ext_ref[:, cells_lon : cells_lon + depth, :cells_lat] = east_ref[...]
    ext_ref[:, cells_lon + depth :, :cells_lat] = west_ref[...]
    ext_ref[:, :, cells_lat : cells_lat + depth] = north_ref[...]
    ext_ref[:, :, lanes - depth :] = south_ref[...]

    def next_col(x):
        return pltpu.roll(x, width - 1, 0)

    def next_row(x):
        return pltpu.roll(x, lanes - 1, 1)

    row = lax.broadcasted_iota(jnp.int32, (width, lanes), 1)
    virtual = is_top & (row >= cells_lat) & (row < cells_lat + depth)
    fold_row = is_top & (row == cells_lat - 1)
    south_edge = is_bottom & (row == lanes - 1)
    kappa_e = ext_ref[nfield + nlev]
    kappa_n = ext_ref[nfield + nlev + 1]
    kappa_e = jnp.where(virtual, next_col(kappa_e), kappa_e)
    kappa_up = next_row(kappa_n)
    kappa_n = jnp.where(virtual, kappa_up, jnp.where(fold_row, 0.5 * (kappa_n + kappa_up), kappa_n))
    for lev in range(nlev):
        mask = ext_ref[nfield + lev]
        coef_e = kappa_e * mask * next_col(mask)
        coef_n = jnp.where(south_edge, 0.0, kappa_n * mask * next_row(mask))
        for var in range(nvar):
            plane = var * nlev + lev
            v = ext_ref[plane]
            for sweep in range(STEPS):
                flux_e = coef_e * (next_col(v) - v)
                flux_n = coef_n * (next_row(v) - v)
                v = v + (flux_e - pltpu.roll(flux_e, 1, 0)) + (flux_n - pltpu.roll(flux_n, 1, 1))
            out_ref[plane] = std_ref[plane] * v[:cells_lon, :cells_lat]


def solution(mesh):
    return jax.shard_map(
        per_device,
        mesh=mesh,
        in_specs=(
            P("ens", None, "lon", "lat"),
            P(None, None, "lon", "lat"),
            P(None, "lon", "lat"),
            P("lon", "lat"),
            P("lon", "lat"),
            P(),
        ),
        out_specs=P("ens", None, "lon", "lat"),
        check_vma=False,
    )
```

```python
import jax
import jax.numpy as jnp
from jax import lax
from jax.experimental import pallas as pl
from jax.experimental.pallas import tpu as pltpu
from jax.sharding import PartitionSpec as P

STEPS = 8


AXES = ("lon", "lat")


def exchange(sends):
    groups = {}
    for k, (pairs, x) in enumerate(sends):
        groups.setdefault(tuple(pairs), []).append(k)
    out = [None] * len(sends)
    for pairs, members in groups.items():
        if len(members) == 1:
            out[members[0]] = lax.ppermute(sends[members[0]][1], AXES, list(pairs))
            continue
        flat = jnp.concatenate([sends[k][1].reshape(-1) for k in members])
        got = lax.ppermute(flat, AXES, list(pairs))
        offset = 0
        for k in members:
            size = sends[k][1].size
            out[k] = got[offset : offset + size].reshape(sends[k][1].shape)
            offset += size
    return out


def pairs_from(d_lon, d_lat, lats=None):
    nlon, nlat = lax.axis_size("lon"), lax.axis_size("lat")
    pairs = []
    for lon in range(nlon):
        for lat in range(nlat) if lats is None else lats:
            dst = lat - d_lat
            if 0 <= dst < nlat:
                pairs.append((lon * nlat + lat, ((lon - d_lon) % nlon) * nlat + dst))
    return pairs


def per_device(control, error_std, land_mask, diff_east, diff_north, fold_partner):
    nvar, nlev, cells_lon, cells_lat = control.shape
    depth = STEPS
    nlon = fold_partner.shape[0]
    width = cells_lon + 2 * depth
    rows = cells_lat + 2 * depth
    nfield = nvar * nlev
    lat_index, lat_peers = lax.axis_index("lat"), lax.axis_size("lat")
    is_top = lat_index == lat_peers - 1
    is_bottom = lat_index == 0
    col0 = lax.axis_index("lon") * cells_lon

    field = (error_std * control).reshape(nfield, cells_lon, cells_lat)
    stack = jnp.concatenate(
        [field, land_mask.astype(jnp.float32), diff_east[None], diff_north[None]], axis=0
    )

    nlon_dev = lax.axis_size("lon")
    d = depth
    top = stack[:, :, cells_lat - d :]
    small = nlon_dev <= 16
    west, east = exchange(
        [(pairs_from(-1, 0), stack[:, cells_lon - d :]), (pairs_from(1, 0), stack[:, :d])]
    )
    wide = jnp.concatenate([stack, east, west], axis=1)
    if lat_peers == 2:
        facing = jnp.where(is_top, wide[:, :, :d], wide[:, :, cells_lat - d :])
        sends = [([(k, k ^ 1) for k in range(2 * nlon_dev)], facing)]
    else:
        sends = [
            (pairs_from(0, -1), wide[:, :, cells_lat - d :]),
            (pairs_from(0, 1), wide[:, :, :d]),
        ]
    lat_got = exchange(sends)
    south, north = (lat_got[0], lat_got[0]) if lat_peers == 2 else lat_got

    if small:
        copies = jnp.broadcast_to(top[None], (nlon_dev,) + top.shape)
        strips = lax.all_to_all(copies, "lon", 0, 0)
        gathered = jnp.concatenate([strips[k] for k in range(nlon_dev)], axis=1)
    else:
        gathered = lax.all_gather(top, "lon", axis=1, tiled=True)
    base = 0
    pivot = fold_partner[0]
    first = (pivot - col0 - cells_lon - depth + 1 - base) % nlon
    doubled = jnp.concatenate([gathered[:, :nlon], gathered[:, :width]], axis=1)
    mirror = lax.dynamic_slice_in_dim(doubled, first, width, axis=1)[:, ::-1, ::-1]
    mirror = jnp.concatenate([mirror[:, d:], mirror[:, :d]], axis=1)
    north = jnp.where(is_top, mirror, north)

    lanes = -(-(cells_lat + 2 * d) // 128) * 128
    vmem = pl.BlockSpec(memory_space=pltpu.VMEM)
    out = pl.pallas_call(
        lambda *refs: diffuse_kernel(*refs, nvar=nvar, nlev=nlev, depth=d),
        out_shape=jax.ShapeDtypeStruct((nfield, cells_lon, cells_lat), jnp.float32),
        in_specs=[vmem] * 6,
        out_specs=vmem,
        scratch_shapes=[pltpu.VMEM((stack.shape[0], width, lanes), jnp.float32)],
    )(stack, east, west, north, south, error_std.reshape(nfield, cells_lon, cells_lat))
    return out.reshape(control.shape)


def diffuse_kernel(
    own_ref, east_ref, west_ref, north_ref, south_ref, std_ref, out_ref, ext_ref,
    *, nvar, nlev, depth
):
    nfield = nvar * nlev
    cells_lon, cells_lat = own_ref.shape[1:]
    width, lanes = ext_ref.shape[1], ext_ref.shape[2]
    lat_index = lax.axis_index("lat")
    is_top = lat_index == lax.axis_size("lat") - 1
    is_bottom = lat_index == 0
    ext_ref[:, :, cells_lat:] = jnp.zeros((ext_ref.shape[0], width, lanes - cells_lat), jnp.float32)
    ext_ref[:, :cells_lon, :cells_lat] = own_ref[...]
    ext_ref[:, cells_lon : cells_lon + depth, :cells_lat] = east_ref[...]
    ext_ref[:, cells_lon + depth :, :cells_lat] = west_ref[...]
    ext_ref[:, :, cells_lat : cells_lat + depth] = north_ref[...]
    ext_ref[:, :, lanes - depth :] = south_ref[...]

    def next_col(x):
        return pltpu.roll(x, width - 1, 0)

    def next_row(x):
        return pltpu.roll(x, lanes - 1, 1)

    row = lax.broadcasted_iota(jnp.int32, (width, lanes), 1)
    virtual = is_top & (row >= cells_lat) & (row < cells_lat + depth)
    fold_row = is_top & (row == cells_lat - 1)
    south_edge = is_bottom & (row == lanes - 1)
    kappa_e = ext_ref[nfield + nlev]
    kappa_n = ext_ref[nfield + nlev + 1]
    kappa_e = jnp.where(virtual, next_col(kappa_e), kappa_e)
    kappa_up = next_row(kappa_n)
    kappa_n = jnp.where(virtual, kappa_up, jnp.where(fold_row, 0.5 * (kappa_n + kappa_up), kappa_n))
    for lev in range(nlev):
        mask = ext_ref[nfield + lev]
        coef_e = kappa_e * mask * next_col(mask)
        coef_n = jnp.where(south_edge, 0.0, kappa_n * mask * next_row(mask))
        for var in range(nvar):
            plane = var * nlev + lev
            v = ext_ref[plane]
            for sweep in range(STEPS):
                flux_e = coef_e * (next_col(v) - v)
                flux_n = coef_n * (next_row(v) - v)
                v = v + (flux_e - pltpu.roll(flux_e, 1, 0)) + (flux_n - pltpu.roll(flux_n, 1, 1))
            out_ref[plane] = std_ref[plane] * v[:cells_lon, :cells_lat]


def solution(mesh):
    return jax.shard_map(
        per_device,
        mesh=mesh,
        in_specs=(
            P("ens", None, "lon", "lat"),
            P(None, None, "lon", "lat"),
            P(None, "lon", "lat"),
            P("lon", "lat"),
            P("lon", "lat"),
            P(),
        ),
        out_specs=P("ens", None, "lon", "lat"),
        check_vma=False,
    )
```

```python
import jax
import jax.numpy as jnp
from jax import lax
from jax.experimental import pallas as pl
from jax.experimental.pallas import tpu as pltpu
from jax.sharding import PartitionSpec as P

STEPS = 8


AXES = ("lon", "lat")


def exchange(sends):
    groups = {}
    for k, (pairs, x) in enumerate(sends):
        groups.setdefault(tuple(pairs), []).append(k)
    out = [None] * len(sends)
    for pairs, members in groups.items():
        if len(members) == 1:
            out[members[0]] = lax.ppermute(sends[members[0]][1], AXES, list(pairs))
            continue
        flat = jnp.concatenate([sends[k][1].reshape(-1) for k in members])
        got = lax.ppermute(flat, AXES, list(pairs))
        offset = 0
        for k in members:
            size = sends[k][1].size
            out[k] = got[offset : offset + size].reshape(sends[k][1].shape)
            offset += size
    return out


def pairs_from(d_lon, d_lat, lats=None):
    nlon, nlat = lax.axis_size("lon"), lax.axis_size("lat")
    pairs = []
    for lon in range(nlon):
        for lat in range(nlat) if lats is None else lats:
            dst = lat - d_lat
            if 0 <= dst < nlat:
                pairs.append((lon * nlat + lat, ((lon - d_lon) % nlon) * nlat + dst))
    return pairs


def per_device(control, error_std, land_mask, diff_east, diff_north, fold_partner):
    nvar, nlev, cells_lon, cells_lat = control.shape
    depth = STEPS
    nlon = fold_partner.shape[0]
    width = cells_lon + 2 * depth
    rows = cells_lat + 2 * depth
    nfield = nvar * nlev
    lat_index, lat_peers = lax.axis_index("lat"), lax.axis_size("lat")
    is_top = lat_index == lat_peers - 1
    is_bottom = lat_index == 0
    col0 = lax.axis_index("lon") * cells_lon

    vmem = pl.BlockSpec(memory_space=pltpu.VMEM)
    stack = pl.pallas_call(
        pack_kernel,
        out_shape=jax.ShapeDtypeStruct((nfield + nlev + 2, cells_lon, cells_lat), jnp.float32),
        in_specs=[vmem] * 5,
        out_specs=vmem,
    )(
        control.reshape(nfield, cells_lon, cells_lat),
        error_std.reshape(nfield, cells_lon, cells_lat),
        land_mask,
        diff_east,
        diff_north,
    )

    nlon_dev = lax.axis_size("lon")
    d = depth
    top = stack[:, :, cells_lat - d :]
    small = nlon_dev <= 16
    west, east = exchange(
        [(pairs_from(-1, 0), stack[:, cells_lon - d :]), (pairs_from(1, 0), stack[:, :d])]
    )
    wide = jnp.concatenate([stack, east, west], axis=1)
    if lat_peers == 2:
        facing = jnp.where(is_top, wide[:, :, :d], wide[:, :, cells_lat - d :])
        sends = [([(k, k ^ 1) for k in range(2 * nlon_dev)], facing)]
    else:
        sends = [
            (pairs_from(0, -1), wide[:, :, cells_lat - d :]),
            (pairs_from(0, 1), wide[:, :, :d]),
        ]
    lat_got = exchange(sends)
    south, north = (lat_got[0], lat_got[0]) if lat_peers == 2 else lat_got

    if small:
        copies = jnp.broadcast_to(top[None], (nlon_dev,) + top.shape)
        strips = lax.all_to_all(copies, "lon", 0, 0)
        gathered = jnp.concatenate([strips[k] for k in range(nlon_dev)], axis=1)
    else:
        gathered = lax.all_gather(top, "lon", axis=1, tiled=True)
    base = 0
    pivot = fold_partner[0]
    first = (pivot - col0 - cells_lon - depth + 1 - base) % nlon
    doubled = jnp.concatenate([gathered[:, :nlon], gathered[:, :width]], axis=1)
    mirror = lax.dynamic_slice_in_dim(doubled, first, width, axis=1)[:, ::-1, ::-1]
    mirror = jnp.concatenate([mirror[:, d:], mirror[:, :d]], axis=1)
    north = jnp.where(is_top, mirror, north)

    lanes = -(-(cells_lat + 2 * d) // 128) * 128
    flags = jnp.stack([is_top, is_bottom]).astype(jnp.int32)
    out = pl.pallas_call(
        lambda *refs: diffuse_kernel(*refs, nvar=nvar, nlev=nlev, depth=d),
        out_shape=jax.ShapeDtypeStruct((nfield, cells_lon, cells_lat), jnp.float32),
        in_specs=[pl.BlockSpec(memory_space=pltpu.SMEM)] + [vmem] * 6,
        out_specs=vmem,
        scratch_shapes=[pltpu.VMEM((stack.shape[0], width, lanes), jnp.float32)],
    )(flags, stack, east, west, north, south, error_std.reshape(nfield, cells_lon, cells_lat))
    return out.reshape(control.shape)


def pack_kernel(control_ref, std_ref, mask_ref, kappa_e_ref, kappa_n_ref, stack_ref):
    nfield, nlev = control_ref.shape[0], mask_ref.shape[0]
    stack_ref[:nfield] = std_ref[...] * control_ref[...]
    stack_ref[nfield : nfield + nlev] = mask_ref[...].astype(jnp.float32)
    stack_ref[nfield + nlev] = kappa_e_ref[...]
    stack_ref[nfield + nlev + 1] = kappa_n_ref[...]


def diffuse_kernel(
    flags_ref, own_ref, east_ref, west_ref, north_ref, south_ref, std_ref, out_ref, ext_ref,
    *, nvar, nlev, depth
):
    nfield = nvar * nlev
    cells_lon, cells_lat = own_ref.shape[1:]
    width, lanes = ext_ref.shape[1], ext_ref.shape[2]
    is_top = flags_ref[0] == 1
    is_bottom = flags_ref[1] == 1
    ext_ref[:, :, cells_lat:] = jnp.zeros((ext_ref.shape[0], width, lanes - cells_lat), jnp.float32)
    ext_ref[:, :cells_lon, :cells_lat] = own_ref[...]
    ext_ref[:, cells_lon : cells_lon + depth, :cells_lat] = east_ref[...]
    ext_ref[:, cells_lon + depth :, :cells_lat] = west_ref[...]
    ext_ref[:, :, cells_lat : cells_lat + depth] = north_ref[...]
    ext_ref[:, :, lanes - depth :] = south_ref[...]

    def next_col(x):
        return pltpu.roll(x, width - 1, 0)

    def next_row(x):
        return pltpu.roll(x, lanes - 1, 1)

    row = lax.broadcasted_iota(jnp.int32, (width, lanes), 1)
    virtual = is_top & (row >= cells_lat) & (row < cells_lat + depth)
    fold_row = is_top & (row == cells_lat - 1)
    south_edge = is_bottom & (row == lanes - 1)
    kappa_e = ext_ref[nfield + nlev]
    kappa_n = ext_ref[nfield + nlev + 1]
    kappa_e = jnp.where(virtual, next_col(kappa_e), kappa_e)
    kappa_up = next_row(kappa_n)
    kappa_n = jnp.where(virtual, kappa_up, jnp.where(fold_row, 0.5 * (kappa_n + kappa_up), kappa_n))
    for lev in range(nlev):
        mask = ext_ref[nfield + lev]
        coef_e = kappa_e * mask * next_col(mask)
        coef_n = jnp.where(south_edge, 0.0, kappa_n * mask * next_row(mask))
        for var in range(nvar):
            plane = var * nlev + lev
            v = ext_ref[plane]
            for sweep in range(STEPS):
                flux_e = coef_e * (next_col(v) - v)
                flux_n = coef_n * (next_row(v) - v)
                v = v + (flux_e - pltpu.roll(flux_e, 1, 0)) + (flux_n - pltpu.roll(flux_n, 1, 1))
            out_ref[plane] = std_ref[plane] * v[:cells_lon, :cells_lat]


def solution(mesh):
    return jax.shard_map(
        per_device,
        mesh=mesh,
        in_specs=(
            P("ens", None, "lon", "lat"),
            P(None, None, "lon", "lat"),
            P(None, "lon", "lat"),
            P("lon", "lat"),
            P("lon", "lat"),
            P(),
        ),
        out_specs=P("ens", None, "lon", "lat"),
        check_vma=False,
    )
```
